512 devices in a mesh: seq: 32 (over z, core), tensor: 16 (over y, x).
Axes of the slice: x: 4, y: 4, z: 16, core: 2. Of those that a mesh axis runs over, the one named last changes fastest.
Arguments:
- hidden: bfloat16 [4, 64, 5120], P(None, None, 'seq'), may hold values from -400 to 400
- norm_gain: bfloat16 [5120], P('seq'), may hold values from 0.099609375 to 1.8984375
- w_qkv: bfloat16 [5120, 7168], P('seq', 'tensor'), may hold values from -0.078125 to 0.078125
- b_qkv: bfloat16 [7168], P('tensor'), may hold values from -3 to 3
- w_out: bfloat16 [5120, 5120], P('tensor', 'seq'), may hold values from -0.078125 to 0.078125
- prefix_key_cache: bfloat16 [16, 12288, 1024], P('tensor', 'seq'), may hold values from -140 to 140
- prefix_value_cache: bfloat16 [16, 12288, 1024], P('tensor', 'seq'), may hold values from -6 to 6
- suffix_key_cache: bfloat16 [64, 4096, 1024], P('tensor', 'seq'), may hold values from -8 to 8
- suffix_value_cache: bfloat16 [64, 4096, 1024], P('tensor', 'seq'), may hold values from -6 to 6
- prefix_lens: int32 [16], P('tensor'), may hold values from 1 to 12288, as said below
- suffix_lens: int32 [64], P('tensor'), may hold values from 0 to 4096, as said below
Outputs:
- attn_out: float32 [4, 64, 5120], P(None, 'tensor', 'seq')
- new_keys: float32 [64, 4, 1024], P('tensor')
- new_values: float32 [64, 4, 1024], P('tensor')
The draws below stay inside these ranges and needn't reach their ends.
Inputs may be any that keep to these rules, and one draw needn't show every extreme that they name: `prefix_lens`: some group has exactly 12288 live slots and some exactly one. `suffix_lens`: some request has exactly 4096 live slots and some none.
All inputs are finite; a program needn't handle non-finite values.
Results may differ from the reference program's by a relative error of at most 0.012.
The reference program's roundings to bfloat16 on the way count: a program that leaves them out, or rounds other values in their place, can miss the bound.
Values may be sent and summed in bfloat16 or wider, within the bound.
No kernel may reach another device: no remote copies, remote signals or barrier semaphores. Data moves between devices by JAX's collectives and lax.ppermute only.
A program may use at most 64 MiB of HBM per device.

```python
import jax
import jax.numpy as jnp
from jax import lax

D = 5120
QUERY_HEADS = 40
KEY_HEADS = 8
HEAD_SIZE = 128
GROUP_REQUESTS = 4
DECODE_STEPS = 4
PREFIX_GROUPS = 16
REQUEST_TOTAL = 64
PREFIX_SLOTS = 12288
SUFFIX_SLOTS = 4096
QW = 5120
KEY_COLUMNS = 1024
QKVW = 7168


def draw_hidden(key, part):
    first, second, third = jax.random.split(key, 3)
    shape = (DECODE_STEPS, REQUEST_TOTAL, D)
    values = jnp.clip(jax.random.normal(first, shape, jnp.float32), -4.0, 4.0)
    scales = jnp.exp(jax.random.uniform(second, (DECODE_STEPS, REQUEST_TOTAL, 1), jnp.float32, 0.0, jnp.log(10.0)))
    column = lax.broadcasted_iota(jnp.int32, (1, 1, D), 2).astype(jnp.float32)
    columns = jnp.exp(column * (jnp.log(3.0) / D)) * jnp.exp(jax.random.uniform(third, (1, 1, D), jnp.float32, 0.0, jnp.log(2.0)))
    return (values * scales * columns).astype(jnp.bfloat16)


def draw_prefix_key_cache(key, part):
    first = jax.random.fold_in(key, 0)
    shape = (PREFIX_GROUPS, PREFIX_SLOTS, KEY_COLUMNS)
    base = 2.0 * jnp.clip(jax.random.normal(first, shape, jnp.float32), -4.0, 4.0)
    return base.astype(jnp.bfloat16)


def draw_prefix_lens(key, part):
    first, second = jax.random.split(key, 2)
    lengths = jax.random.randint(first, (PREFIX_GROUPS,), 1, PREFIX_SLOTS + 1)
    longest = jax.random.randint(second, (), 0, PREFIX_GROUPS)
    places = jnp.arange(PREFIX_GROUPS, dtype=jnp.int32)
    lengths = jnp.where(places == longest, PREFIX_SLOTS, lengths)
    lengths = jnp.where(places == (longest + 1) % PREFIX_GROUPS, 1, lengths)
    return lengths.astype(jnp.int32)


def draw_suffix_lens(key, part):
    first, second = jax.random.split(key, 2)
    lengths = jax.random.randint(first, (REQUEST_TOTAL,), 0, SUFFIX_SLOTS + 1)
    longest = jax.random.randint(second, (), 0, REQUEST_TOTAL)
    places = jnp.arange(REQUEST_TOTAL, dtype=jnp.int32)
    lengths = jnp.where(places == longest, SUFFIX_SLOTS, lengths)
    lengths = jnp.where(places == (longest + 1) % REQUEST_TOTAL, 0, lengths)
    return lengths.astype(jnp.int32)


def steps_of(stream_key, shape, shards, low, high):
    def one(position, blocks):
        heights = jax.random.uniform(jax.random.fold_in(jax.random.fold_in(stream_key, 6), position), (blocks,), jnp.float32, low / len(shards), high / len(shards))
        return jnp.repeat(jnp.exp(heights), shape[position] // blocks).reshape((-1,) + (1,) * (len(shape) - position - 1))

    factor_of = one(*shards[0])
    for cut in shards[1:]:
        factor_of = factor_of * one(*cut)
    return factor_of


def noise(key, extent, width, most, cuts=(), kind=jnp.bfloat16):
    values = jax.random.normal(key, extent, jnp.float32) * width
    if len(cuts) > 0:
        values = steps_of(key, extent, cuts, -0.22, 0.18) * values
    return jnp.clip(values, min=-most, max=most).astype(kind)


def setup_inputs(seed: int = 0) -> dict:
    key_list = jax.random.split(jax.random.key(seed), 12)
    hidden = draw_hidden(jax.random.fold_in(key_list[11], 71), 0)
    norm_gain = jnp.clip(1.0 + 0.18 * jax.random.normal(key_list[1], (D,), jnp.float32), 0.099609375, 1.8984375).astype(jnp.bfloat16)
    w_qkv = noise(key_list[2], (D, QKVW), D ** -0.5, 0.078125, ((0, 32), (1, 16)))
    b_qkv = noise(key_list[3], (QKVW,), 0.5, 3.0, ((0, 16),))
    w_out = noise(key_list[4], (QW, D), QW ** -0.5, 0.078125, ((0, 16), (1, 32)))
    prefix_key_cache = draw_prefix_key_cache(jax.random.fold_in(key_list[11], 71), 0)
    prefix_value_cache = noise(key_list[6], (PREFIX_GROUPS, PREFIX_SLOTS, KEY_COLUMNS), 1.0, 6.0, ((0, 16), (1, 32)))
    suffix_key_cache = noise(key_list[7], (REQUEST_TOTAL, SUFFIX_SLOTS, KEY_COLUMNS), 2.0, 8.0, ((0, 16), (1, 32)))
    suffix_value_cache = noise(key_list[8], (REQUEST_TOTAL, SUFFIX_SLOTS, KEY_COLUMNS), 1.0, 6.0, ((0, 16), (1, 32)))
    prefix_lens = draw_prefix_lens(jax.random.fold_in(key_list[11], 71), 0)
    suffix_lens = draw_suffix_lens(jax.random.fold_in(key_list[11], 71), 0)
    return dict(hidden=hidden, norm_gain=norm_gain, w_qkv=w_qkv, b_qkv=b_qkv, w_out=w_out, prefix_key_cache=prefix_key_cache, prefix_value_cache=prefix_value_cache, suffix_key_cache=suffix_key_cache, suffix_value_cache=suffix_value_cache, prefix_lens=prefix_lens, suffix_lens=suffix_lens)


epsilon = 1e-06
masked_fill = -1e+30

def apply_rotary(values, token_positions):
    half = values.shape[-1] // 2
    freq = jnp.exp(-(jnp.arange(half, dtype=jnp.float32) * (2.0 / values.shape[-1])) * jnp.log(jnp.float32(1000000.0)))
    angles = token_positions[..., None, None] * freq
    cosine = jnp.cos(angles)
    sine = jnp.sin(angles)
    left = values[..., :half]
    right = values[..., half:]
    return jnp.concatenate([left * cosine - right * sine, right * cosine + left * sine], axis=-1)

def rounded(weights):
    return lax.optimization_barrier(weights.astype(jnp.bfloat16)).astype(jnp.float32)

def reference(hidden, norm_gain, w_qkv, b_qkv, w_out, prefix_key_cache, prefix_value_cache, suffix_key_cache, suffix_value_cache, prefix_lens, suffix_lens):
    query_group_width = QUERY_HEADS // KEY_HEADS
    query_width = QUERY_HEADS * HEAD_SIZE
    query_rows = DECODE_STEPS * query_group_width
    scale = float(HEAD_SIZE) ** (-0.5)
    xf = hidden.astype(jnp.float32)
    mean_sq = lax.optimization_barrier(jnp.mean(xf * xf, axis=2, keepdims=True))
    normed = (xf * lax.rsqrt(mean_sq + epsilon) * norm_gain.astype(jnp.float32)).astype(jnp.bfloat16)
    combined_output = jnp.dot(normed.reshape(DECODE_STEPS * REQUEST_TOTAL, D), w_qkv, preferred_element_type=jnp.float32)
    combined_output = combined_output.reshape(DECODE_STEPS, REQUEST_TOTAL, QKVW) + b_qkv.astype(jnp.float32)
    owners = (jnp.arange(REQUEST_TOTAL) // GROUP_REQUESTS).astype(jnp.int32)
    token_positions = (prefix_lens[owners] + suffix_lens)[None, :] + jnp.arange(DECODE_STEPS, dtype=jnp.int32)[:, None]
    token_positions = token_positions.astype(jnp.float32)
    query_matrix = apply_rotary(combined_output[..., :query_width].reshape(DECODE_STEPS, REQUEST_TOTAL, QUERY_HEADS, HEAD_SIZE), token_positions).astype(jnp.bfloat16)
    keys_float = apply_rotary(combined_output[..., query_width:query_width + KEY_COLUMNS].reshape(DECODE_STEPS, REQUEST_TOTAL, KEY_HEADS, HEAD_SIZE), token_positions)
    values_float = combined_output[..., query_width + KEY_COLUMNS:].reshape(DECODE_STEPS, REQUEST_TOTAL, KEY_HEADS, HEAD_SIZE)
    current_keys = keys_float.astype(jnp.bfloat16)
    current_values = values_float.astype(jnp.bfloat16)
    new_keys = keys_float.reshape(DECODE_STEPS, REQUEST_TOTAL, KEY_COLUMNS).transpose(1, 0, 2)
    new_values = values_float.reshape(DECODE_STEPS, REQUEST_TOTAL, KEY_COLUMNS).transpose(1, 0, 2)
    query_by_group = query_matrix.reshape(DECODE_STEPS, PREFIX_GROUPS, GROUP_REQUESTS, KEY_HEADS, query_group_width, HEAD_SIZE).transpose(1, 2, 3, 0, 4, 5).reshape(PREFIX_GROUPS, GROUP_REQUESTS, KEY_HEADS, query_rows, HEAD_SIZE)
    key_by_group = current_keys.reshape(DECODE_STEPS, PREFIX_GROUPS, GROUP_REQUESTS, KEY_HEADS, HEAD_SIZE).transpose(1, 2, 3, 0, 4)
    value_by_group = current_values.reshape(DECODE_STEPS, PREFIX_GROUPS, GROUP_REQUESTS, KEY_HEADS, HEAD_SIZE).transpose(1, 2, 3, 0, 4)
    prefix_key_rows = prefix_key_cache.reshape(PREFIX_GROUPS, PREFIX_SLOTS, KEY_HEADS, HEAD_SIZE)
    prefix_value_rows = prefix_value_cache.reshape(PREFIX_GROUPS, PREFIX_SLOTS, KEY_HEADS, HEAD_SIZE)
    suffix_key_rows = suffix_key_cache.reshape(PREFIX_GROUPS, GROUP_REQUESTS, SUFFIX_SLOTS, KEY_HEADS, HEAD_SIZE)
    suffix_value_rows = suffix_value_cache.reshape(PREFIX_GROUPS, GROUP_REQUESTS, SUFFIX_SLOTS, KEY_HEADS, HEAD_SIZE)
    suffix_group = suffix_lens.reshape(PREFIX_GROUPS, GROUP_REQUESTS)

    def attend(items):
        query_blk, prefix_key_block, prefix_value_block, suffix_key_block, suffix_value_block, fresh_k, fresh_v, pre_len, suf_len = items
        query_f = query_blk.astype(jnp.float32)
        score_pre = jnp.einsum('rhqd,phd->rhqp', query_f, prefix_key_block.astype(jnp.float32)) * scale
        score_suf = jnp.einsum('rhqd,rshd->rhqs', query_f, suffix_key_block.astype(jnp.float32)) * scale
        score_new = jnp.einsum('rhqd,rhid->rhqi', query_f, fresh_k.astype(jnp.float32)) * scale
        pre_mask = (jnp.arange(PREFIX_SLOTS, dtype=jnp.int32) < pre_len)[None, None, None, :]
        suf_mask = (jnp.arange(SUFFIX_SLOTS, dtype=jnp.int32)[None, :] < suf_len[:, None])[:, None, None, :]
        new_mask = ((jnp.arange(query_rows, dtype=jnp.int32) // query_group_width)[:, None] >= jnp.arange(DECODE_STEPS, dtype=jnp.int32)[None, :])[None, None]
        fill_pre = jnp.where(pre_mask, score_pre, masked_fill)
        fill_suf = jnp.where(suf_mask, score_suf, masked_fill)
        fill_new = jnp.where(new_mask, score_new, masked_fill)
        top = jnp.maximum(jnp.maximum(lax.optimization_barrier(jnp.max(fill_pre, axis=3)), lax.optimization_barrier(jnp.max(fill_suf, axis=3))), lax.optimization_barrier(jnp.max(fill_new, axis=3)))[..., None]
        prob_pre = jnp.where(pre_mask, jnp.exp(fill_pre - top), 0.0)
        prob_suf = jnp.where(suf_mask, jnp.exp(fill_suf - top), 0.0)
        prob_new = jnp.where(new_mask, jnp.exp(fill_new - top), 0.0)
        total = lax.optimization_barrier(jnp.sum(prob_pre, axis=3)) + lax.optimization_barrier(jnp.sum(prob_suf, axis=3)) + lax.optimization_barrier(jnp.sum(prob_new, axis=3))
        summed = jnp.einsum('rhqp,phd->rhqd', rounded(prob_pre), prefix_value_block.astype(jnp.float32))
        summed = summed + jnp.einsum('rhqs,rshd->rhqd', rounded(prob_suf), suffix_value_block.astype(jnp.float32))
        summed = summed + jnp.einsum('rhqi,rhid->rhqd', rounded(prob_new), fresh_v.astype(jnp.float32))
        return (summed / total[..., None]).astype(jnp.bfloat16)
    attention_output = lax.map(attend, (query_by_group, prefix_key_rows, prefix_value_rows, suffix_key_rows, suffix_value_rows, key_by_group, value_by_group, prefix_lens, suffix_group))
    head_count = attention_output.reshape(PREFIX_GROUPS, GROUP_REQUESTS, KEY_HEADS, DECODE_STEPS, query_group_width, HEAD_SIZE).transpose(3, 0, 1, 2, 4, 5).reshape(DECODE_STEPS * REQUEST_TOTAL, query_width)
    attn_out = jnp.dot(head_count, w_out, preferred_element_type=jnp.float32).reshape(DECODE_STEPS, REQUEST_TOTAL, D)
    return (attn_out, new_keys, new_values)
```

```python
import jax
import jax.numpy as jnp
from jax import lax
from jax.sharding import PartitionSpec as P

D = 5120
QUERY_HEADS = 40
KEY_HEADS = 8
HEAD_SIZE = 128
KEY_COLUMNS = 1024


epsilon = 1e-06
masked_fill = -1e30


def apply_rotary(values, token_positions):
    half = values.shape[-1] // 2
    freq = jnp.exp(
        -(jnp.arange(half, dtype=jnp.float32) * (2.0 / values.shape[-1]))
        * jnp.log(jnp.float32(1000000.0))
    )
    angles = token_positions[..., None, None] * freq
    cosine = jnp.cos(angles)
    sine = jnp.sin(angles)
    left = values[..., :half]
    right = values[..., half:]
    return jnp.concatenate([left * cosine - right * sine, right * cosine + left * sine], axis=-1)


def body(
    hidden,
    norm_gain,
    w_qkv,
    b_qkv,
    w_out,
    prefix_key_cache,
    prefix_value_cache,
    suffix_key_cache,
    suffix_value_cache,
    prefix_lens,
    suffix_lens,
):
    seq_count = lax.axis_size("seq")
    tensor_count = lax.axis_size("tensor")
    steps = hidden.shape[0]
    request_total = hidden.shape[1]
    requests = suffix_lens.shape[0]
    columns = w_qkv.shape[1]
    prefix_count = prefix_key_cache.shape[1]
    suffix_count = suffix_key_cache.shape[1]
    query_group_width = QUERY_HEADS // KEY_HEADS
    query_width = QUERY_HEADS * HEAD_SIZE
    query_rows = steps * query_group_width
    scale = float(HEAD_SIZE) ** (-0.5)
    seq_index = lax.axis_index("seq")

    w_out_cols = lax.all_gather(w_out, "tensor", axis=0, tiled=True)

    xf = hidden.astype(jnp.float32)
    local_squares = jnp.sum(xf * xf, axis=2)
    squares = jnp.sum(
        lax.all_to_all(
            jnp.broadcast_to(local_squares[None], (seq_count,) + local_squares.shape),
            "seq", 0, 0, tiled=True,
        ),
        axis=0,
    )
    normed = (
        xf * lax.rsqrt(squares / D + epsilon)[..., None] * norm_gain.astype(jnp.float32)
    ).astype(jnp.bfloat16)
    partial_value = jnp.einsum("sbd,dc->sbc", normed, w_qkv, preferred_element_type=jnp.float32)

    halves = seq_count // (steps * requests)
    half_width = columns // halves
    groups = request_total // requests
    chunks = (
        partial_value.reshape(steps, groups, requests, halves, half_width)
        .transpose(0, 2, 3, 1, 4)
        .reshape(seq_count, groups, half_width)
    )
    reduced = jnp.sum(lax.all_to_all(chunks, "seq", 0, 0, tiled=True), axis=0)
    bias = lax.dynamic_slice_in_dim(
        b_qkv.astype(jnp.float32), (seq_index % halves) * half_width, half_width
    )
    reduced = reduced + bias[None, :]
    owned_rows = lax.all_to_all(reduced, "tensor", 0, 0, tiled=True)
    gathered = lax.all_gather(owned_rows, "seq", axis=0, tiled=False)
    combined_output = (
        gathered.reshape(steps, requests, halves, tensor_count, half_width)
        .transpose(0, 1, 3, 2, 4)
        .reshape(steps, requests, tensor_count * columns)
    )

    token_positions = (
        (prefix_lens[0] + suffix_lens)[None, :]
        + jnp.arange(steps, dtype=jnp.int32)[:, None]
    ).astype(jnp.float32)
    query_matrix = apply_rotary(
        combined_output[..., :query_width].reshape(steps, requests, QUERY_HEADS, HEAD_SIZE),
        token_positions,
    ).astype(jnp.bfloat16)
    keys_float = apply_rotary(
        combined_output[..., query_width : query_width + KEY_COLUMNS].reshape(
            steps, requests, KEY_HEADS, HEAD_SIZE
        ),
        token_positions,
    )
    values_float = combined_output[..., query_width + KEY_COLUMNS :].reshape(
        steps, requests, KEY_HEADS, HEAD_SIZE
    )
    current_keys = keys_float.astype(jnp.bfloat16)
    current_values = values_float.astype(jnp.bfloat16)
    new_keys = keys_float.reshape(steps, requests, KEY_COLUMNS).transpose(1, 0, 2)
    new_values = values_float.reshape(steps, requests, KEY_COLUMNS).transpose(1, 0, 2)
    query_by_group = (
        query_matrix.reshape(steps, requests, KEY_HEADS, query_group_width, HEAD_SIZE)
        .transpose(1, 2, 0, 3, 4)
        .reshape(requests, KEY_HEADS, query_rows, HEAD_SIZE)
    )

    prefix_key_block = prefix_key_cache[0].reshape(prefix_count, KEY_HEADS, HEAD_SIZE)
    prefix_value_block = prefix_value_cache[0].reshape(prefix_count, KEY_HEADS, HEAD_SIZE)
    suffix_key_block = suffix_key_cache.reshape(requests, suffix_count, KEY_HEADS, HEAD_SIZE)
    suffix_value_block = suffix_value_cache.reshape(requests, suffix_count, KEY_HEADS, HEAD_SIZE)
    score_pre = (
        jnp.einsum(
            "rhqd,phd->rhqp", query_by_group, prefix_key_block, preferred_element_type=jnp.float32
        )
        * scale
    )
    score_suf = (
        jnp.einsum(
            "rhqd,rshd->rhqs", query_by_group, suffix_key_block, preferred_element_type=jnp.float32
        )
        * scale
    )
    pre_mask = (
        seq_index * prefix_count + jnp.arange(prefix_count, dtype=jnp.int32) < prefix_lens[0]
    )[None, None, None, :]
    suf_mask = (
        (seq_index * suffix_count + jnp.arange(suffix_count, dtype=jnp.int32))[None, :]
        < suffix_lens[:, None]
    )[:, None, None, :]
    fill_pre = jnp.where(pre_mask, score_pre, masked_fill)
    fill_suf = jnp.where(suf_mask, score_suf, masked_fill)
    local_max = jnp.maximum(jnp.max(fill_pre, axis=3), jnp.max(fill_suf, axis=3))
    prob_pre = jnp.where(pre_mask, jnp.exp(fill_pre - local_max[..., None]), 0.0)
    prob_suf = jnp.where(suf_mask, jnp.exp(fill_suf - local_max[..., None]), 0.0)
    local_weight = jnp.sum(prob_pre, axis=3) + jnp.sum(prob_suf, axis=3)
    local_acc = jnp.einsum(
        "rhqp,phd->rhqd",
        prob_pre.astype(jnp.bfloat16),
        prefix_value_block,
        preferred_element_type=jnp.float32,
    )
    local_acc = local_acc + jnp.einsum(
        "rhqs,rshd->rhqd",
        prob_suf.astype(jnp.bfloat16),
        suffix_value_block,
        preferred_element_type=jnp.float32,
    )

    fresh_k = current_keys.transpose(1, 2, 0, 3)
    fresh_v = current_values.transpose(1, 2, 0, 3)
    score_new = (
        jnp.einsum("rhqd,rhid->rhqi", query_by_group, fresh_k, preferred_element_type=jnp.float32)
        * scale
    )
    new_mask = (
        (jnp.arange(query_rows, dtype=jnp.int32) // query_group_width)[:, None]
        >= jnp.arange(steps, dtype=jnp.int32)[None, :]
    )[None, None]
    fill_new = jnp.where(new_mask, score_new, masked_fill)
    new_max = jnp.max(fill_new, axis=3)
    prob_new = jnp.where(new_mask, jnp.exp(fill_new - new_max[..., None]), 0.0)
    new_weight = jnp.sum(prob_new, axis=3)
    new_acc = jnp.einsum(
        "rhqi,rhid->rhqd",
        prob_new.astype(jnp.bfloat16),
        fresh_v,
        preferred_element_type=jnp.float32,
    )

    packed = jnp.concatenate(
        [local_acc, local_max[..., None], local_weight[..., None]], axis=-1
    ).reshape(seq_count, query_rows, HEAD_SIZE + 2)
    arrived = lax.all_to_all(packed, "seq", 0, 0, tiled=True)
    part_acc = arrived[..., :HEAD_SIZE]
    part_max = arrived[..., HEAD_SIZE]
    part_weight = arrived[..., HEAD_SIZE + 1]
    global_max = jnp.max(part_max, axis=0)
    factor = jnp.exp(part_max - global_max[None])
    global_weight = jnp.sum(part_weight * factor, axis=0)
    global_acc = jnp.sum(part_acc * factor[..., None], axis=0)

    mine_r = seq_index // KEY_HEADS
    mine_h = seq_index % KEY_HEADS
    own_new_max = new_max[mine_r, mine_h]
    own_new_weight = new_weight[mine_r, mine_h]
    own_new_acc = new_acc[mine_r, mine_h]
    top = jnp.maximum(global_max, own_new_max)
    factor_old = jnp.exp(global_max - top)
    factor_new = jnp.exp(own_new_max - top)
    total = global_weight * factor_old + own_new_weight * factor_new
    summed = global_acc * factor_old[..., None] + own_new_acc * factor_new[..., None]
    attention_slice = (summed / total[..., None]).astype(jnp.bfloat16)

    attention_all = lax.all_gather(attention_slice, "seq", axis=0, tiled=False)
    heads_local = (
        attention_all.reshape(requests, KEY_HEADS, steps, query_group_width, HEAD_SIZE)
        .transpose(2, 0, 1, 3, 4)
        .reshape(steps, requests, query_width)
    )
    owned = jnp.einsum("sbc,cd->sbd", heads_local, w_out_cols, preferred_element_type=jnp.float32)
    return (owned, new_keys, new_values)


def solution(mesh):
    placed = (
        P(None, None, "seq"),
        P("seq"),
        P("seq", "tensor"),
        P("tensor"),
        P("tensor", "seq"),
        P("tensor", "seq", None),
        P("tensor", "seq", None),
        P("tensor", "seq", None),
        P("tensor", "seq", None),
        P("tensor"),
        P("tensor"),
    )
    return jax.shard_map(
        body,
        mesh=mesh,
        in_specs=placed,
        out_specs=(P(None, "tensor", "seq"), P("tensor", None, None), P("tensor", None, None)),
        check_vma=False,
    )
```

```python
import jax
import jax.numpy as jnp
from jax import lax
from jax.sharding import PartitionSpec as P

D = 5120
QUERY_HEADS = 40
KEY_HEADS = 8
HEAD_SIZE = 128
KEY_COLUMNS = 1024


epsilon = 1e-06
masked_fill = -1e30


def apply_rotary(values, token_positions):
    half = values.shape[-1] // 2
    freq = jnp.exp(
        -(jnp.arange(half, dtype=jnp.float32) * (2.0 / values.shape[-1]))
        * jnp.log(jnp.float32(1000000.0))
    )
    angles = token_positions[..., None, None] * freq
    cosine = jnp.cos(angles)
    sine = jnp.sin(angles)
    left = values[..., :half]
    right = values[..., half:]
    return jnp.concatenate([left * cosine - right * sine, right * cosine + left * sine], axis=-1)


def broadcast_gather(block, axis):
    count = lax.axis_size(axis)
    return lax.all_to_all(
        jnp.broadcast_to(block[None], (count,) + block.shape), axis, 0, 0, tiled=True
    )


def body(
    hidden,
    norm_gain,
    w_qkv,
    b_qkv,
    w_out,
    prefix_key_cache,
    prefix_value_cache,
    suffix_key_cache,
    suffix_value_cache,
    prefix_lens,
    suffix_lens,
):
    seq_count = lax.axis_size("seq")
    tensor_count = lax.axis_size("tensor")
    steps = hidden.shape[0]
    request_total = hidden.shape[1]
    requests = suffix_lens.shape[0]
    columns = w_qkv.shape[1]
    prefix_count = prefix_key_cache.shape[1]
    suffix_count = suffix_key_cache.shape[1]
    query_group_width = QUERY_HEADS // KEY_HEADS
    query_width = QUERY_HEADS * HEAD_SIZE
    query_rows = steps * query_group_width
    scale = float(HEAD_SIZE) ** (-0.5)
    seq_index = lax.axis_index("seq")

    w_out_cols = broadcast_gather(w_out, "tensor").reshape(-1, w_out.shape[1])

    xf = hidden.astype(jnp.float32)
    local_squares = jnp.sum(xf * xf, axis=2)
    squares = jnp.sum(
        lax.all_to_all(
            jnp.broadcast_to(local_squares[None], (seq_count,) + local_squares.shape),
            "seq", 0, 0, tiled=True,
        ),
        axis=0,
    )
    normed = (
        xf * lax.rsqrt(squares / D + epsilon)[..., None] * norm_gain.astype(jnp.float32)
    ).astype(jnp.bfloat16)
    partial_value = jnp.einsum("sbd,dc->sbc", normed, w_qkv, preferred_element_type=jnp.float32)

    halves = seq_count // (steps * requests)
    half_width = columns // halves
    groups = request_total // requests
    chunks = (
        partial_value.reshape(steps, groups, requests, halves, half_width)
        .transpose(0, 2, 3, 1, 4)
        .reshape(seq_count, groups, half_width)
    )
    reduced = jnp.sum(lax.all_to_all(chunks, "seq", 0, 0, tiled=True), axis=0)
    bias = lax.dynamic_slice_in_dim(
        b_qkv.astype(jnp.float32), (seq_index % halves) * half_width, half_width
    )
    reduced = reduced + bias[None, :]
    owned_rows = lax.all_to_all(reduced, "tensor", 0, 0, tiled=True)
    gathered = broadcast_gather(owned_rows, "seq")
    combined_output = (
        gathered.reshape(steps, requests, halves, tensor_count, half_width)
        .transpose(0, 1, 3, 2, 4)
        .reshape(steps, requests, tensor_count * columns)
    )

    token_positions = (
        (prefix_lens[0] + suffix_lens)[None, :]
        + jnp.arange(steps, dtype=jnp.int32)[:, None]
    ).astype(jnp.float32)
    query_matrix = apply_rotary(
        combined_output[..., :query_width].reshape(steps, requests, QUERY_HEADS, HEAD_SIZE),
        token_positions,
    ).astype(jnp.bfloat16)
    keys_float = apply_rotary(
        combined_output[..., query_width : query_width + KEY_COLUMNS].reshape(
            steps, requests, KEY_HEADS, HEAD_SIZE
        ),
        token_positions,
    )
    values_float = combined_output[..., query_width + KEY_COLUMNS :].reshape(
        steps, requests, KEY_HEADS, HEAD_SIZE
    )
    current_keys = keys_float.astype(jnp.bfloat16)
    current_values = values_float.astype(jnp.bfloat16)
    new_keys = keys_float.reshape(steps, requests, KEY_COLUMNS).transpose(1, 0, 2)
    new_values = values_float.reshape(steps, requests, KEY_COLUMNS).transpose(1, 0, 2)
    query_by_group = (
        query_matrix.reshape(steps, requests, KEY_HEADS, query_group_width, HEAD_SIZE)
        .transpose(1, 2, 0, 3, 4)
        .reshape(requests, KEY_HEADS, query_rows, HEAD_SIZE)
    )

    prefix_key_block = prefix_key_cache[0].reshape(prefix_count, KEY_HEADS, HEAD_SIZE)
    prefix_value_block = prefix_value_cache[0].reshape(prefix_count, KEY_HEADS, HEAD_SIZE)
    suffix_key_block = suffix_key_cache.reshape(requests, suffix_count, KEY_HEADS, HEAD_SIZE)
    suffix_value_block = suffix_value_cache.reshape(requests, suffix_count, KEY_HEADS, HEAD_SIZE)
    score_pre = (
        jnp.einsum(
            "rhqd,phd->rhqp", query_by_group, prefix_key_block, preferred_element_type=jnp.float32
        )
        * scale
    )
    score_suf = (
        jnp.einsum(
            "rhqd,rshd->rhqs", query_by_group, suffix_key_block, preferred_element_type=jnp.float32
        )
        * scale
    )
    pre_mask = (
        seq_index * prefix_count + jnp.arange(prefix_count, dtype=jnp.int32) < prefix_lens[0]
    )[None, None, None, :]
    suf_mask = (
        (seq_index * suffix_count + jnp.arange(suffix_count, dtype=jnp.int32))[None, :]
        < suffix_lens[:, None]
    )[:, None, None, :]
    fill_pre = jnp.where(pre_mask, score_pre, masked_fill)
    fill_suf = jnp.where(suf_mask, score_suf, masked_fill)
    local_max = jnp.maximum(jnp.max(fill_pre, axis=3), jnp.max(fill_suf, axis=3))
    prob_pre = jnp.where(pre_mask, jnp.exp(fill_pre - local_max[..., None]), 0.0)
    prob_suf = jnp.where(suf_mask, jnp.exp(fill_suf - local_max[..., None]), 0.0)
    local_weight = jnp.sum(prob_pre, axis=3) + jnp.sum(prob_suf, axis=3)
    local_acc = jnp.einsum(
        "rhqp,phd->rhqd",
        prob_pre.astype(jnp.bfloat16),
        prefix_value_block,
        preferred_element_type=jnp.float32,
    )
    local_acc = local_acc + jnp.einsum(
        "rhqs,rshd->rhqd",
        prob_suf.astype(jnp.bfloat16),
        suffix_value_block,
        preferred_element_type=jnp.float32,
    )

    fresh_k = current_keys.transpose(1, 2, 0, 3)
    fresh_v = current_values.transpose(1, 2, 0, 3)
    score_new = (
        jnp.einsum("rhqd,rhid->rhqi", query_by_group, fresh_k, preferred_element_type=jnp.float32)
        * scale
    )
    new_mask = (
        (jnp.arange(query_rows, dtype=jnp.int32) // query_group_width)[:, None]
        >= jnp.arange(steps, dtype=jnp.int32)[None, :]
    )[None, None]
    fill_new = jnp.where(new_mask, score_new, masked_fill)
    new_max = jnp.max(fill_new, axis=3)
    prob_new = jnp.where(new_mask, jnp.exp(fill_new - new_max[..., None]), 0.0)
    new_weight = jnp.sum(prob_new, axis=3)
    new_acc = jnp.einsum(
        "rhqi,rhid->rhqd",
        prob_new.astype(jnp.bfloat16),
        fresh_v,
        preferred_element_type=jnp.float32,
    )

    packed = jnp.concatenate(
        [local_acc, local_max[..., None], local_weight[..., None]], axis=-1
    ).reshape(seq_count, query_rows, HEAD_SIZE + 2)
    arrived = lax.all_to_all(packed, "seq", 0, 0, tiled=True)
    part_acc = arrived[..., :HEAD_SIZE]
    part_max = arrived[..., HEAD_SIZE]
    part_weight = arrived[..., HEAD_SIZE + 1]
    global_max = jnp.max(part_max, axis=0)
    factor = jnp.exp(part_max - global_max[None])
    global_weight = jnp.sum(part_weight * factor, axis=0)
    global_acc = jnp.sum(part_acc * factor[..., None], axis=0)

    mine_r = seq_index // KEY_HEADS
    mine_h = seq_index % KEY_HEADS
    own_new_max = new_max[mine_r, mine_h]
    own_new_weight = new_weight[mine_r, mine_h]
    own_new_acc = new_acc[mine_r, mine_h]
    top = jnp.maximum(global_max, own_new_max)
    factor_old = jnp.exp(global_max - top)
    factor_new = jnp.exp(own_new_max - top)
    total = global_weight * factor_old + own_new_weight * factor_new
    summed = global_acc * factor_old[..., None] + own_new_acc * factor_new[..., None]
    attention_slice = (summed / total[..., None]).astype(jnp.bfloat16)

    attention_all = broadcast_gather(attention_slice, "seq")
    heads_local = (
        attention_all.reshape(requests, KEY_HEADS, steps, query_group_width, HEAD_SIZE)
        .transpose(2, 0, 1, 3, 4)
        .reshape(steps, requests, query_width)
    )
    owned = jnp.einsum("sbc,cd->sbd", heads_local, w_out_cols, preferred_element_type=jnp.float32)
    return (owned, new_keys, new_values)


def solution(mesh):
    placed = (
        P(None, None, "seq"),
        P("seq"),
        P("seq", "tensor"),
        P("tensor"),
        P("tensor", "seq"),
        P("tensor", "seq", None),
        P("tensor", "seq", None),
        P("tensor", "seq", None),
        P("tensor", "seq", None),
        P("tensor"),
        P("tensor"),
    )
    return jax.shard_map(
        body,
        mesh=mesh,
        in_specs=placed,
        out_specs=(P(None, "tensor", "seq"), P("tensor", None, None), P("tensor", None, None)),
        check_vma=False,
    )
```

```python
import jax
import jax.numpy as jnp
from jax import lax
from jax.sharding import PartitionSpec as P

D = 5120
QUERY_HEADS = 40
KEY_HEADS = 8
HEAD_SIZE = 128
KEY_COLUMNS = 1024


SEQ = ("z", "core")
epsilon = 1e-06
masked_fill = -1e30


def apply_rotary(values, token_positions):
    half = values.shape[-1] // 2
    freq = jnp.exp(
        -(jnp.arange(half, dtype=jnp.float32) * (2.0 / values.shape[-1]))
        * jnp.log(jnp.float32(1000000.0))
    )
    angles = token_positions[..., None, None] * freq
    cosine = jnp.cos(angles)
    sine = jnp.sin(angles)
    left = values[..., :half]
    right = values[..., half:]
    return jnp.concatenate([left * cosine - right * sine, right * cosine + left * sine], axis=-1)


def body(
    hidden,
    norm_gain,
    w_qkv,
    b_qkv,
    w_out,
    prefix_key_cache,
    prefix_value_cache,
    suffix_key_cache,
    suffix_value_cache,
    prefix_lens,
    suffix_lens,
):
    seq_count = lax.axis_size(SEQ)
    tensor_count = lax.axis_size("tensor")
    steps = hidden.shape[0]
    request_total = hidden.shape[1]
    requests = suffix_lens.shape[0]
    columns = w_qkv.shape[1]
    prefix_count = prefix_key_cache.shape[1]
    suffix_count = suffix_key_cache.shape[1]
    query_group_width = QUERY_HEADS // KEY_HEADS
    query_width = QUERY_HEADS * HEAD_SIZE
    query_rows = steps * query_group_width
    scale = float(HEAD_SIZE) ** (-0.5)
    seq_index = lax.axis_index(SEQ)

    w_out_cols = lax.all_gather(w_out, "tensor", axis=0, tiled=True)

    xf = hidden.astype(jnp.float32)
    local_squares = jnp.sum(xf * xf, axis=2)
    squares = jnp.sum(
        lax.all_to_all(
            jnp.broadcast_to(local_squares[None], (seq_count,) + local_squares.shape),
            SEQ, 0, 0, tiled=True,
        ),
        axis=0,
    )
    normed = (
        xf * lax.rsqrt(squares / D + epsilon)[..., None] * norm_gain.astype(jnp.float32)
    ).astype(jnp.bfloat16)
    partial_value = jnp.einsum("sbd,dc->sbc", normed, w_qkv, preferred_element_type=jnp.float32)

    halves = seq_count // (steps * requests)
    half_width = columns // halves
    groups = request_total // requests
    core = lax.axis_index("core")
    plane_count = seq_count // halves
    by_half = partial_value.reshape(steps, groups, requests, halves, half_width)
    keep = lax.dynamic_index_in_dim(by_half, core, axis=3, keepdims=False)
    send = lax.dynamic_index_in_dim(by_half, 1 - core, axis=3, keepdims=False)
    pair_sum = keep + lax.ppermute(send, "core", [(0, 1), (1, 0)])
    chunks = pair_sum.transpose(0, 2, 1, 3).reshape(plane_count, groups, half_width)
    reduced = jnp.sum(lax.all_to_all(chunks, "z", 0, 0, tiled=True), axis=0)
    bias = lax.dynamic_slice_in_dim(
        b_qkv.astype(jnp.float32), (seq_index % halves) * half_width, half_width
    )
    reduced = reduced + bias[None, :]
    owned_rows = lax.all_to_all(reduced, "tensor", 0, 0, tiled=True)
    gathered = lax.all_gather(owned_rows, SEQ, axis=0, tiled=False)
    combined_output = (
        gathered.reshape(steps, requests, halves, tensor_count, half_width)
        .transpose(0, 1, 3, 2, 4)
        .reshape(steps, requests, tensor_count * columns)
    )

    token_positions = (
        (prefix_lens[0] + suffix_lens)[None, :]
        + jnp.arange(steps, dtype=jnp.int32)[:, None]
    ).astype(jnp.float32)
    query_matrix = apply_rotary(
        combined_output[..., :query_width].reshape(steps, requests, QUERY_HEADS, HEAD_SIZE),
        token_positions,
    ).astype(jnp.bfloat16)
    keys_float = apply_rotary(
        combined_output[..., query_width : query_width + KEY_COLUMNS].reshape(
            steps, requests, KEY_HEADS, HEAD_SIZE
        ),
        token_positions,
    )
    values_float = combined_output[..., query_width + KEY_COLUMNS :].reshape(
        steps, requests, KEY_HEADS, HEAD_SIZE
    )
    current_keys = keys_float.astype(jnp.bfloat16)
    current_values = values_float.astype(jnp.bfloat16)
    new_keys = keys_float.reshape(steps, requests, KEY_COLUMNS).transpose(1, 0, 2)
    new_values = values_float.reshape(steps, requests, KEY_COLUMNS).transpose(1, 0, 2)
    query_by_group = (
        query_matrix.reshape(steps, requests, KEY_HEADS, query_group_width, HEAD_SIZE)
        .transpose(1, 2, 0, 3, 4)
        .reshape(requests, KEY_HEADS, query_rows, HEAD_SIZE)
    )

    prefix_key_block = prefix_key_cache[0].reshape(prefix_count, KEY_HEADS, HEAD_SIZE)
    prefix_value_block = prefix_value_cache[0].reshape(prefix_count, KEY_HEADS, HEAD_SIZE)
    suffix_key_block = suffix_key_cache.reshape(requests, suffix_count, KEY_HEADS, HEAD_SIZE)
    suffix_value_block = suffix_value_cache.reshape(requests, suffix_count, KEY_HEADS, HEAD_SIZE)
    score_pre = (
        jnp.einsum(
            "rhqd,phd->rhqp", query_by_group, prefix_key_block, preferred_element_type=jnp.float32
        )
        * scale
    )
    score_suf = (
        jnp.einsum(
            "rhqd,rshd->rhqs", query_by_group, suffix_key_block, preferred_element_type=jnp.float32
        )
        * scale
    )
    pre_mask = (
        seq_index * prefix_count + jnp.arange(prefix_count, dtype=jnp.int32) < prefix_lens[0]
    )[None, None, None, :]
    suf_mask = (
        (seq_index * suffix_count + jnp.arange(suffix_count, dtype=jnp.int32))[None, :]
        < suffix_lens[:, None]
    )[:, None, None, :]
    fill_pre = jnp.where(pre_mask, score_pre, masked_fill)
    fill_suf = jnp.where(suf_mask, score_suf, masked_fill)
    local_max = jnp.maximum(jnp.max(fill_pre, axis=3), jnp.max(fill_suf, axis=3))
    prob_pre = jnp.where(pre_mask, jnp.exp(fill_pre - local_max[..., None]), 0.0)
    prob_suf = jnp.where(suf_mask, jnp.exp(fill_suf - local_max[..., None]), 0.0)
    local_weight = jnp.sum(prob_pre, axis=3) + jnp.sum(prob_suf, axis=3)
    local_acc = jnp.einsum(
        "rhqp,phd->rhqd",
        prob_pre.astype(jnp.bfloat16),
        prefix_value_block,
        preferred_element_type=jnp.float32,
    )
    local_acc = local_acc + jnp.einsum(
        "rhqs,rshd->rhqd",
        prob_suf.astype(jnp.bfloat16),
        suffix_value_block,
        preferred_element_type=jnp.float32,
    )

    fresh_k = current_keys.transpose(1, 2, 0, 3)
    fresh_v = current_values.transpose(1, 2, 0, 3)
    score_new = (
        jnp.einsum("rhqd,rhid->rhqi", query_by_group, fresh_k, preferred_element_type=jnp.float32)
        * scale
    )
    new_mask = (
        (jnp.arange(query_rows, dtype=jnp.int32) // query_group_width)[:, None]
        >= jnp.arange(steps, dtype=jnp.int32)[None, :]
    )[None, None]
    fill_new = jnp.where(new_mask, score_new, masked_fill)
    new_max = jnp.max(fill_new, axis=3)
    prob_new = jnp.where(new_mask, jnp.exp(fill_new - new_max[..., None]), 0.0)
    new_weight = jnp.sum(prob_new, axis=3)
    new_acc = jnp.einsum(
        "rhqi,rhid->rhqd",
        prob_new.astype(jnp.bfloat16),
        fresh_v,
        preferred_element_type=jnp.float32,
    )

    packed = jnp.concatenate(
        [local_acc, local_max[..., None], local_weight[..., None]], axis=-1
    ).reshape(requests, KEY_HEADS // 2, 2, query_rows, HEAD_SIZE + 2)
    keep = lax.dynamic_index_in_dim(packed, core, axis=2, keepdims=False)
    came = lax.ppermute(
        lax.dynamic_index_in_dim(packed, 1 - core, axis=2, keepdims=False), "core", [(0, 1), (1, 0)]
    )
    pair_max = jnp.maximum(keep[..., HEAD_SIZE], came[..., HEAD_SIZE])
    keep_factor = jnp.exp(keep[..., HEAD_SIZE] - pair_max)
    came_factor = jnp.exp(came[..., HEAD_SIZE] - pair_max)
    pair_weight = keep[..., HEAD_SIZE + 1] * keep_factor + came[..., HEAD_SIZE + 1] * came_factor
    pair_acc = keep[..., :HEAD_SIZE] * keep_factor[..., None] + came[..., :HEAD_SIZE] * came_factor[..., None]
    pair_packed = jnp.concatenate(
        [pair_acc, pair_max[..., None], pair_weight[..., None]], axis=-1
    ).reshape(seq_count // 2, query_rows, HEAD_SIZE + 2)
    arrived = lax.all_to_all(pair_packed, "z", 0, 0, tiled=True)
    part_acc = arrived[..., :HEAD_SIZE]
    part_max = arrived[..., HEAD_SIZE]
    part_weight = arrived[..., HEAD_SIZE + 1]
    global_max = jnp.max(part_max, axis=0)
    factor = jnp.exp(part_max - global_max[None])
    global_weight = jnp.sum(part_weight * factor, axis=0)
    global_acc = jnp.sum(part_acc * factor[..., None], axis=0)

    mine_r = seq_index // KEY_HEADS
    mine_h = seq_index % KEY_HEADS
    own_new_max = new_max[mine_r, mine_h]
    own_new_weight = new_weight[mine_r, mine_h]
    own_new_acc = new_acc[mine_r, mine_h]
    top = jnp.maximum(global_max, own_new_max)
    factor_old = jnp.exp(global_max - top)
    factor_new = jnp.exp(own_new_max - top)
    total = global_weight * factor_old + own_new_weight * factor_new
    summed = global_acc * factor_old[..., None] + own_new_acc * factor_new[..., None]
    attention_slice = (summed / total[..., None]).astype(jnp.bfloat16)

    attention_all = lax.all_gather(attention_slice, SEQ, axis=0, tiled=False)
    heads_local = (
        attention_all.reshape(requests, KEY_HEADS, steps, query_group_width, HEAD_SIZE)
        .transpose(2, 0, 1, 3, 4)
        .reshape(steps, requests, query_width)
    )
    owned = jnp.einsum("sbc,cd->sbd", heads_local, w_out_cols, preferred_element_type=jnp.float32)
    return (owned, new_keys, new_values)


def solution(mesh):
    placed = (
        P(None, None, SEQ),
        P(SEQ),
        P(SEQ, "tensor"),
        P("tensor"),
        P("tensor", SEQ),
        P("tensor", SEQ, None),
        P("tensor", SEQ, None),
        P("tensor", SEQ, None),
        P("tensor", SEQ, None),
        P("tensor"),
        P("tensor"),
    )
    planes = jax.sharding.Mesh(
        mesh.devices.reshape(-1, 2, mesh.devices.shape[1]), ("z", "core", "tensor")
    )
    return jax.shard_map(
        body,
        mesh=planes,
        in_specs=placed,
        out_specs=(P(None, "tensor", ("z", "core")), P("tensor", None, None), P("tensor", None, None)),
        check_vma=False,
    )
```

```python
import jax
import jax.numpy as jnp
from jax import lax
from jax.sharding import PartitionSpec as P

D = 5120
QUERY_HEADS = 40
KEY_HEADS = 8
HEAD_SIZE = 128
KEY_COLUMNS = 1024


SEQ = ("z", "core")
epsilon = 1e-06
masked_fill = -1e30


def apply_rotary(values, token_positions):
    half = values.shape[-1] // 2
    freq = jnp.exp(
        -(jnp.arange(half, dtype=jnp.float32) * (2.0 / values.shape[-1]))
        * jnp.log(jnp.float32(1000000.0))
    )
    angles = token_positions[..., None, None] * freq
    cosine = jnp.cos(angles)
    sine = jnp.sin(angles)
    left = values[..., :half]
    right = values[..., half:]
    return jnp.concatenate([left * cosine - right * sine, right * cosine + left * sine], axis=-1)


def body(
    hidden,
    norm_gain,
    w_qkv,
    b_qkv,
    w_out,
    prefix_key_cache,
    prefix_value_cache,
    suffix_key_cache,
    suffix_value_cache,
    prefix_lens,
    suffix_lens,
):
    seq_count = lax.axis_size(SEQ)
    tensor_count = lax.axis_size("tensor")
    steps = hidden.shape[0]
    request_total = hidden.shape[1]
    requests = suffix_lens.shape[0]
    columns = w_qkv.shape[1]
    prefix_count = prefix_key_cache.shape[1]
    suffix_count = suffix_key_cache.shape[1]
    query_group_width = QUERY_HEADS // KEY_HEADS
    query_width = QUERY_HEADS * HEAD_SIZE
    query_rows = steps * query_group_width
    scale = float(HEAD_SIZE) ** (-0.5)
    seq_index = lax.axis_index(SEQ)

    w_out_cols = lax.all_gather(w_out, "tensor", axis=0, tiled=True)

    xf = hidden.astype(jnp.float32)
    local_squares = jnp.sum(xf * xf, axis=2)
    squares = jnp.sum(
        lax.all_to_all(
            jnp.broadcast_to(local_squares[None], (seq_count,) + local_squares.shape),
            SEQ, 0, 0, tiled=True,
        ),
        axis=0,
    )
    normed = (
        xf * lax.rsqrt(squares / D + epsilon)[..., None] * norm_gain.astype(jnp.float32)
    ).astype(jnp.bfloat16)
    partial_value = jnp.einsum("sbd,dc->sbc", normed, w_qkv, preferred_element_type=jnp.float32)

    halves = seq_count // (steps * requests)
    half_width = columns // halves
    groups = request_total // requests
    core = lax.axis_index("core")
    plane_count = seq_count // halves
    by_half = partial_value.reshape(steps, groups, requests, halves, half_width)
    keep = lax.dynamic_index_in_dim(by_half, core, axis=3, keepdims=False)
    send = lax.dynamic_index_in_dim(by_half, 1 - core, axis=3, keepdims=False)
    pair_sum = keep + lax.ppermute(send, "core", [(0, 1), (1, 0)])
    chunks = pair_sum.transpose(0, 2, 1, 3).reshape(plane_count, groups, half_width)
    reduced = jnp.sum(lax.all_to_all(chunks, "z", 0, 0, tiled=True), axis=0)
    bias = lax.dynamic_slice_in_dim(
        b_qkv.astype(jnp.float32), (seq_index % halves) * half_width, half_width
    )
    reduced = reduced + bias[None, :]
    owned_rows = lax.all_to_all(reduced, "tensor", 0, 0, tiled=True)
    gathered = lax.all_gather(owned_rows, SEQ, axis=0, tiled=False)
    combined_output = (
        gathered.reshape(steps, requests, halves, tensor_count, half_width)
        .transpose(0, 1, 3, 2, 4)
        .reshape(steps, requests, tensor_count * columns)
    )

    token_positions = (
        (prefix_lens[0] + suffix_lens)[None, :]
        + jnp.arange(steps, dtype=jnp.int32)[:, None]
    ).astype(jnp.float32)
    query_matrix = apply_rotary(
        combined_output[..., :query_width].reshape(steps, requests, QUERY_HEADS, HEAD_SIZE),
        token_positions,
    ).astype(jnp.bfloat16)
    keys_float = apply_rotary(
        combined_output[..., query_width : query_width + KEY_COLUMNS].reshape(
            steps, requests, KEY_HEADS, HEAD_SIZE
        ),
        token_positions,
    )
    values_float = combined_output[..., query_width + KEY_COLUMNS :].reshape(
        steps, requests, KEY_HEADS, HEAD_SIZE
    )
    current_keys = keys_float.astype(jnp.bfloat16)
    current_values = values_float.astype(jnp.bfloat16)
    new_keys = keys_float.reshape(steps, requests, KEY_COLUMNS).transpose(1, 0, 2)
    new_values = values_float.reshape(steps, requests, KEY_COLUMNS).transpose(1, 0, 2)
    query_by_group = (
        query_matrix.reshape(steps, requests, KEY_HEADS, query_group_width, HEAD_SIZE)
        .transpose(1, 2, 0, 3, 4)
        .reshape(requests, KEY_HEADS, query_rows, HEAD_SIZE)
    )
    w_out_cols, query_by_group = lax.optimization_barrier((w_out_cols, query_by_group))

    prefix_key_block = prefix_key_cache[0].reshape(prefix_count, KEY_HEADS, HEAD_SIZE)
    prefix_value_block = prefix_value_cache[0].reshape(prefix_count, KEY_HEADS, HEAD_SIZE)
    suffix_key_block = suffix_key_cache.reshape(requests, suffix_count, KEY_HEADS, HEAD_SIZE)
    suffix_value_block = suffix_value_cache.reshape(requests, suffix_count, KEY_HEADS, HEAD_SIZE)
    score_pre = (
        jnp.einsum(
            "rhqd,phd->rhqp", query_by_group, prefix_key_block, preferred_element_type=jnp.float32
        )
        * scale
    )
    score_suf = (
        jnp.einsum(
            "rhqd,rshd->rhqs", query_by_group, suffix_key_block, preferred_element_type=jnp.float32
        )
        * scale
    )
    pre_mask = (
        seq_index * prefix_count + jnp.arange(prefix_count, dtype=jnp.int32) < prefix_lens[0]
    )[None, None, None, :]
    suf_mask = (
        (seq_index * suffix_count + jnp.arange(suffix_count, dtype=jnp.int32))[None, :]
        < suffix_lens[:, None]
    )[:, None, None, :]
    fill_pre = jnp.where(pre_mask, score_pre, masked_fill)
    fill_suf = jnp.where(suf_mask, score_suf, masked_fill)
    local_max = jnp.maximum(jnp.max(fill_pre, axis=3), jnp.max(fill_suf, axis=3))
    prob_pre = jnp.where(pre_mask, jnp.exp(fill_pre - local_max[..., None]), 0.0)
    prob_suf = jnp.where(suf_mask, jnp.exp(fill_suf - local_max[..., None]), 0.0)
    local_weight = jnp.sum(prob_pre, axis=3) + jnp.sum(prob_suf, axis=3)
    local_acc = jnp.einsum(
        "rhqp,phd->rhqd",
        prob_pre.astype(jnp.bfloat16),
        prefix_value_block,
        preferred_element_type=jnp.float32,
    )
    local_acc = local_acc + jnp.einsum(
        "rhqs,rshd->rhqd",
        prob_suf.astype(jnp.bfloat16),
        suffix_value_block,
        preferred_element_type=jnp.float32,
    )

    fresh_k = current_keys.transpose(1, 2, 0, 3)
    fresh_v = current_values.transpose(1, 2, 0, 3)
    score_new = (
        jnp.einsum("rhqd,rhid->rhqi", query_by_group, fresh_k, preferred_element_type=jnp.float32)
        * scale
    )
    new_mask = (
        (jnp.arange(query_rows, dtype=jnp.int32) // query_group_width)[:, None]
        >= jnp.arange(steps, dtype=jnp.int32)[None, :]
    )[None, None]
    fill_new = jnp.where(new_mask, score_new, masked_fill)
    new_max = jnp.max(fill_new, axis=3)
    prob_new = jnp.where(new_mask, jnp.exp(fill_new - new_max[..., None]), 0.0)
    new_weight = jnp.sum(prob_new, axis=3)
    new_acc = jnp.einsum(
        "rhqi,rhid->rhqd",
        prob_new.astype(jnp.bfloat16),
        fresh_v,
        preferred_element_type=jnp.float32,
    )

    lane_pad = ((0, 0), (0, 0), (0, HEAD_SIZE - query_rows))
    packed = jnp.concatenate(
        [
            local_acc,
            jnp.pad(local_max, lane_pad)[:, :, None, :],
            jnp.pad(local_weight, lane_pad)[:, :, None, :],
        ],
        axis=2,
    ).reshape(requests, KEY_HEADS // 2, 2, query_rows + 2, HEAD_SIZE)
    keep = lax.dynamic_index_in_dim(packed, core, axis=2, keepdims=False)
    came = lax.ppermute(
        lax.dynamic_index_in_dim(packed, 1 - core, axis=2, keepdims=False), "core", [(0, 1), (1, 0)]
    )
    keep_max = keep[..., query_rows, :query_rows]
    came_max = came[..., query_rows, :query_rows]
    pair_max = jnp.maximum(keep_max, came_max)
    keep_factor = jnp.exp(keep_max - pair_max)
    came_factor = jnp.exp(came_max - pair_max)
    pair_weight = (
        keep[..., query_rows + 1, :query_rows] * keep_factor
        + came[..., query_rows + 1, :query_rows] * came_factor
    )
    pair_acc = (
        keep[..., :query_rows, :] * keep_factor[..., None]
        + came[..., :query_rows, :] * came_factor[..., None]
    )
    pad_rows = ((0, 0), (0, 0), (0, HEAD_SIZE - query_rows))
    pair_packed = jnp.concatenate(
        [
            pair_acc,
            jnp.pad(pair_max, pad_rows)[:, :, None, :],
            jnp.pad(pair_weight, pad_rows)[:, :, None, :],
        ],
        axis=2,
    ).reshape(seq_count // 2, query_rows + 2, HEAD_SIZE)
    arrived = lax.all_to_all(pair_packed, "z", 0, 0, tiled=True)
    part_acc = arrived[:, :query_rows, :]
    part_max = arrived[:, query_rows, :query_rows]
    part_weight = arrived[:, query_rows + 1, :query_rows]
    global_max = jnp.max(part_max, axis=0)
    factor = jnp.exp(part_max - global_max[None])
    global_weight = jnp.sum(part_weight * factor, axis=0)
    global_acc = jnp.sum(part_acc * factor[..., None], axis=0)

    mine_r = seq_index // KEY_HEADS
    mine_h = seq_index % KEY_HEADS
    own_new_max = new_max[mine_r, mine_h]
    own_new_weight = new_weight[mine_r, mine_h]
    own_new_acc = new_acc[mine_r, mine_h]
    top = jnp.maximum(global_max, own_new_max)
    factor_old = jnp.exp(global_max - top)
    factor_new = jnp.exp(own_new_max - top)
    total = global_weight * factor_old + own_new_weight * factor_new
    summed = global_acc * factor_old[..., None] + own_new_acc * factor_new[..., None]
    attention_slice = (summed / total[..., None]).astype(jnp.bfloat16)

    attention_all = lax.all_gather(attention_slice, SEQ, axis=0, tiled=False)
    heads_local = (
        attention_all.reshape(requests, KEY_HEADS, steps, query_group_width, HEAD_SIZE)
        .transpose(2, 0, 1, 3, 4)
        .reshape(steps, requests, query_width)
    )
    owned = jnp.einsum("sbc,cd->sbd", heads_local, w_out_cols, preferred_element_type=jnp.float32)
    return (owned, new_keys, new_values)


def solution(mesh):
    placed = (
        P(None, None, SEQ),
        P(SEQ),
        P(SEQ, "tensor"),
        P("tensor"),
        P("tensor", SEQ),
        P("tensor", SEQ, None),
        P("tensor", SEQ, None),
        P("tensor", SEQ, None),
        P("tensor", SEQ, None),
        P("tensor"),
        P("tensor"),
    )
    planes = jax.sharding.Mesh(
        mesh.devices.reshape(-1, 2, mesh.devices.shape[1]), ("z", "core", "tensor")
    )
    return jax.shard_map(
        body,
        mesh=planes,
        in_specs=placed,
        out_specs=(P(None, "tensor", ("z", "core")), P("tensor", None, None), P("tensor", None, None)),
        check_vma=False,
    )
```

```python
import jax
import jax.numpy as jnp
from jax import lax
from jax.sharding import PartitionSpec as P

D = 5120
QUERY_HEADS = 40
KEY_HEADS = 8
HEAD_SIZE = 128
KEY_COLUMNS = 1024


SEQ = ("z", "core")
epsilon = 1e-06
masked_fill = -1e30


def apply_rotary(values, token_positions):
    half = values.shape[-1] // 2
    freq = jnp.exp(
        -(jnp.arange(half, dtype=jnp.float32) * (2.0 / values.shape[-1]))
        * jnp.log(jnp.float32(1000000.0))
    )
    angles = token_positions[..., None, None] * freq
    cosine = jnp.cos(angles)
    sine = jnp.sin(angles)
    left = values[..., :half]
    right = values[..., half:]
    return jnp.concatenate([left * cosine - right * sine, right * cosine + left * sine], axis=-1)


def body(
    hidden,
    norm_gain,
    w_qkv,
    b_qkv,
    w_out,
    prefix_key_cache,
    prefix_value_cache,
    suffix_key_cache,
    suffix_value_cache,
    prefix_lens,
    suffix_lens,
):
    seq_count = lax.axis_size(SEQ)
    tensor_count = lax.axis_size("tensor")
    steps = hidden.shape[0]
    request_total = hidden.shape[1]
    requests = suffix_lens.shape[0]
    columns = w_qkv.shape[1]
    prefix_count = prefix_key_cache.shape[1]
    suffix_count = suffix_key_cache.shape[1]
    query_group_width = QUERY_HEADS // KEY_HEADS
    query_width = QUERY_HEADS * HEAD_SIZE
    query_rows = steps * query_group_width
    scale = float(HEAD_SIZE) ** (-0.5)
    seq_index = lax.axis_index(SEQ)

    w_out_cols = lax.all_gather(w_out, "tensor", axis=0, tiled=True)

    xf = hidden.astype(jnp.float32)
    local_squares = jnp.sum(xf * xf, axis=2)
    squares = jnp.sum(
        lax.all_to_all(
            jnp.broadcast_to(local_squares[None], (seq_count,) + local_squares.shape),
            SEQ, 0, 0, tiled=True,
        ),
        axis=0,
    )
    normed = (
        xf * lax.rsqrt(squares / D + epsilon)[..., None] * norm_gain.astype(jnp.float32)
    ).astype(jnp.bfloat16)
    partial_value = jnp.einsum("sbd,dc->sbc", normed, w_qkv, preferred_element_type=jnp.float32)

    halves = seq_count // (steps * requests)
    half_width = columns // halves
    groups = request_total // requests
    core = lax.axis_index("core")
    plane_count = seq_count // halves
    by_half = partial_value.reshape(steps, groups, requests, halves, half_width)
    keep = lax.dynamic_index_in_dim(by_half, core, axis=3, keepdims=False)
    send = lax.dynamic_index_in_dim(by_half, 1 - core, axis=3, keepdims=False)
    pair_sum = keep + lax.ppermute(send, "core", [(0, 1), (1, 0)])
    chunks = pair_sum.transpose(0, 2, 1, 3).reshape(plane_count, groups, half_width)
    reduced = jnp.sum(lax.all_to_all(chunks, "z", 0, 0, tiled=True), axis=0)
    bias = lax.dynamic_slice_in_dim(
        b_qkv.astype(jnp.float32), (seq_index % halves) * half_width, half_width
    )
    reduced = reduced + bias[None, :]
    owned_rows = lax.all_to_all(reduced, "tensor", 0, 0, tiled=True)
    gathered = lax.all_gather(owned_rows, SEQ, axis=0, tiled=False)
    combined_output = (
        gathered.reshape(steps, requests, halves, tensor_count, half_width)
        .transpose(0, 1, 3, 2, 4)
        .reshape(steps, requests, tensor_count * columns)
    )

    token_positions = (
        (prefix_lens[0] + suffix_lens)[None, :]
        + jnp.arange(steps, dtype=jnp.int32)[:, None]
    ).astype(jnp.float32)
    query_matrix = apply_rotary(
        combined_output[..., :query_width].reshape(steps, requests, QUERY_HEADS, HEAD_SIZE),
        token_positions,
    ).astype(jnp.bfloat16)
    keys_float = apply_rotary(
        combined_output[..., query_width : query_width + KEY_COLUMNS].reshape(
            steps, requests, KEY_HEADS, HEAD_SIZE
        ),
        token_positions,
    )
    values_float = combined_output[..., query_width + KEY_COLUMNS :].reshape(
        steps, requests, KEY_HEADS, HEAD_SIZE
    )
    current_keys = keys_float.astype(jnp.bfloat16)
    current_values = values_float.astype(jnp.bfloat16)
    new_keys = keys_float.reshape(steps, requests, KEY_COLUMNS).transpose(1, 0, 2)
    new_values = values_float.reshape(steps, requests, KEY_COLUMNS).transpose(1, 0, 2)
    query_by_group = (
        query_matrix.reshape(steps, requests, KEY_HEADS, query_group_width, HEAD_SIZE)
        .transpose(1, 2, 0, 3, 4)
        .reshape(requests, KEY_HEADS, query_rows, HEAD_SIZE)
    )

    prefix_key_block = prefix_key_cache[0].reshape(prefix_count, KEY_HEADS, HEAD_SIZE)
    prefix_value_block = prefix_value_cache[0].reshape(prefix_count, KEY_HEADS, HEAD_SIZE)
    suffix_key_block = suffix_key_cache.reshape(requests, suffix_count, KEY_HEADS, HEAD_SIZE)
    suffix_value_block = suffix_value_cache.reshape(requests, suffix_count, KEY_HEADS, HEAD_SIZE)
    score_pre = (
        jnp.einsum(
            "rhqd,phd->rhqp", query_by_group, prefix_key_block, preferred_element_type=jnp.float32
        )
        * scale
    )
    score_suf = (
        jnp.einsum(
            "rhqd,rshd->rhqs", query_by_group, suffix_key_block, preferred_element_type=jnp.float32
        )
        * scale
    )
    pre_mask = (
        seq_index * prefix_count + jnp.arange(prefix_count, dtype=jnp.int32) < prefix_lens[0]
    )[None, None, None, :]
    suf_mask = (
        (seq_index * suffix_count + jnp.arange(suffix_count, dtype=jnp.int32))[None, :]
        < suffix_lens[:, None]
    )[:, None, None, :]
    fill_pre = jnp.where(pre_mask, score_pre, masked_fill)
    fill_suf = jnp.where(suf_mask, score_suf, masked_fill)
    local_max = jnp.maximum(jnp.max(fill_pre, axis=3), jnp.max(fill_suf, axis=3))
    prob_pre = jnp.where(pre_mask, jnp.exp(fill_pre - local_max[..., None]), 0.0)
    prob_suf = jnp.where(suf_mask, jnp.exp(fill_suf - local_max[..., None]), 0.0)
    local_weight = jnp.sum(prob_pre, axis=3) + jnp.sum(prob_suf, axis=3)
    local_acc = jnp.einsum(
        "rhqp,phd->rhqd",
        prob_pre.astype(jnp.bfloat16),
        prefix_value_block,
        preferred_element_type=jnp.float32,
    )
    local_acc = local_acc + jnp.einsum(
        "rhqs,rshd->rhqd",
        prob_suf.astype(jnp.bfloat16),
        suffix_value_block,
        preferred_element_type=jnp.float32,
    )

    fresh_k = current_keys.transpose(1, 2, 0, 3)
    fresh_v = current_values.transpose(1, 2, 0, 3)
    score_new = (
        jnp.einsum("rhqd,rhid->rhqi", query_by_group, fresh_k, preferred_element_type=jnp.float32)
        * scale
    )
    new_mask = (
        (jnp.arange(query_rows, dtype=jnp.int32) // query_group_width)[:, None]
        >= jnp.arange(steps, dtype=jnp.int32)[None, :]
    )[None, None]
    fill_new = jnp.where(new_mask, score_new, masked_fill)
    new_max = jnp.max(fill_new, axis=3)
    prob_new = jnp.where(new_mask, jnp.exp(fill_new - new_max[..., None]), 0.0)
    new_weight = jnp.sum(prob_new, axis=3)
    new_acc = jnp.einsum(
        "rhqi,rhid->rhqd",
        prob_new.astype(jnp.bfloat16),
        fresh_v,
        preferred_element_type=jnp.float32,
    )

    lane_pad = ((0, 0), (0, 0), (0, HEAD_SIZE - query_rows))
    packed = jnp.concatenate(
        [
            local_acc,
            jnp.pad(local_max, lane_pad)[:, :, None, :],
            jnp.pad(local_weight, lane_pad)[:, :, None, :],
        ],
        axis=2,
    ).reshape(requests, KEY_HEADS // 2, 2, query_rows + 2, HEAD_SIZE)
    keep = lax.dynamic_index_in_dim(packed, core, axis=2, keepdims=False)
    came = lax.ppermute(
        lax.dynamic_index_in_dim(packed, 1 - core, axis=2, keepdims=False), "core", [(0, 1), (1, 0)]
    )
    keep_max = keep[..., query_rows, :query_rows]
    came_max = came[..., query_rows, :query_rows]
    pair_max = jnp.maximum(keep_max, came_max)
    keep_factor = jnp.exp(keep_max - pair_max)
    came_factor = jnp.exp(came_max - pair_max)
    pair_weight = (
        keep[..., query_rows + 1, :query_rows] * keep_factor
        + came[..., query_rows + 1, :query_rows] * came_factor
    )
    pair_acc = (
        keep[..., :query_rows, :] * keep_factor[..., None]
        + came[..., :query_rows, :] * came_factor[..., None]
    )
    pad_rows = ((0, 0), (0, 0), (0, HEAD_SIZE - query_rows))
    pair_packed = jnp.concatenate(
        [
            pair_acc,
            jnp.pad(pair_max, pad_rows)[:, :, None, :],
            jnp.pad(pair_weight, pad_rows)[:, :, None, :],
        ],
        axis=2,
    ).reshape(seq_count // 2, query_rows + 2, HEAD_SIZE)
    arrived = lax.all_to_all(pair_packed, "z", 0, 0, tiled=True)
    w_out_cols, arrived = lax.optimization_barrier((w_out_cols, arrived))
    part_acc = arrived[:, :query_rows, :]
    part_max = arrived[:, query_rows, :query_rows]
    part_weight = arrived[:, query_rows + 1, :query_rows]
    global_max = jnp.max(part_max, axis=0)
    factor = jnp.exp(part_max - global_max[None])
    global_weight = jnp.sum(part_weight * factor, axis=0)
    global_acc = jnp.sum(part_acc * factor[..., None], axis=0)

    mine_r = seq_index // KEY_HEADS
    mine_h = seq_index % KEY_HEADS
    own_new_max = new_max[mine_r, mine_h]
    own_new_weight = new_weight[mine_r, mine_h]
    own_new_acc = new_acc[mine_r, mine_h]
    top = jnp.maximum(global_max, own_new_max)
    factor_old = jnp.exp(global_max - top)
    factor_new = jnp.exp(own_new_max - top)
    total = global_weight * factor_old + own_new_weight * factor_new
    summed = global_acc * factor_old[..., None] + own_new_acc * factor_new[..., None]
    attention_slice = (summed / total[..., None]).astype(jnp.bfloat16)

    attention_all = lax.all_gather(attention_slice, SEQ, axis=0, tiled=False)
    heads_local = (
        attention_all.reshape(requests, KEY_HEADS, steps, query_group_width, HEAD_SIZE)
        .transpose(2, 0, 1, 3, 4)
        .reshape(steps, requests, query_width)
    )
    owned = jnp.einsum("sbc,cd->sbd", heads_local, w_out_cols, preferred_element_type=jnp.float32)
    return (owned, new_keys, new_values)


def solution(mesh):
    placed = (
        P(None, None, SEQ),
        P(SEQ),
        P(SEQ, "tensor"),
        P("tensor"),
        P("tensor", SEQ),
        P("tensor", SEQ, None),
        P("tensor", SEQ, None),
        P("tensor", SEQ, None),
        P("tensor", SEQ, None),
        P("tensor"),
        P("tensor"),
    )
    planes = jax.sharding.Mesh(
        mesh.devices.reshape(-1, 2, mesh.devices.shape[1]), ("z", "core", "tensor")
    )
    return jax.shard_map(
        body,
        mesh=planes,
        in_specs=placed,
        out_specs=(P(None, "tensor", ("z", "core")), P("tensor", None, None), P("tensor", None, None)),
        check_vma=False,
    )
```

```python
import jax
import jax.numpy as jnp
from jax import lax
from jax.sharding import PartitionSpec as P

D = 5120
QUERY_HEADS = 40
KEY_HEADS = 8
HEAD_SIZE = 128
KEY_COLUMNS = 1024


SEQ = ("z", "core")
epsilon = 1e-06
masked_fill = -1e30


def apply_rotary(values, token_positions):
    half = values.shape[-1] // 2
    freq = jnp.exp(
        -(jnp.arange(half, dtype=jnp.float32) * (2.0 / values.shape[-1]))
        * jnp.log(jnp.float32(1000000.0))
    )
    angles = token_positions[..., None, None] * freq
    cosine = jnp.cos(angles)
    sine = jnp.sin(angles)
    left = values[..., :half]
    right = values[..., half:]
    return jnp.concatenate([left * cosine - right * sine, right * cosine + left * sine], axis=-1)


def body(
    hidden,
    norm_gain,
    w_qkv,
    b_qkv,
    w_out,
    prefix_key_cache,
    prefix_value_cache,
    suffix_key_cache,
    suffix_value_cache,
    prefix_lens,
    suffix_lens,
):
    seq_count = lax.axis_size(SEQ)
    tensor_count = lax.axis_size("tensor")
    steps = hidden.shape[0]
    request_total = hidden.shape[1]
    requests = suffix_lens.shape[0]
    columns = w_qkv.shape[1]
    prefix_count = prefix_key_cache.shape[1]
    suffix_count = suffix_key_cache.shape[1]
    query_group_width = QUERY_HEADS // KEY_HEADS
    query_width = QUERY_HEADS * HEAD_SIZE
    query_rows = steps * query_group_width
    scale = float(HEAD_SIZE) ** (-0.5)
    seq_index = lax.axis_index(SEQ)

    w_out_cols = lax.all_gather(w_out, "tensor", axis=0, tiled=True)

    xf = hidden.astype(jnp.float32)
    local_squares = jnp.sum(xf * xf, axis=2)
    squares = jnp.sum(
        lax.all_to_all(
            jnp.broadcast_to(local_squares[None], (seq_count,) + local_squares.shape),
            SEQ, 0, 0, tiled=True,
        ),
        axis=0,
    )
    normed = (
        xf * lax.rsqrt(squares / D + epsilon)[..., None] * norm_gain.astype(jnp.float32)
    ).astype(jnp.bfloat16)
    partial_value = jnp.einsum("sbd,dc->sbc", normed, w_qkv, preferred_element_type=jnp.float32)

    halves = seq_count // (steps * requests)
    half_width = columns // halves
    groups = request_total // requests
    core = lax.axis_index("core")
    plane_count = seq_count // halves
    by_half = partial_value.reshape(steps, groups, requests, halves, half_width)
    keep = lax.dynamic_index_in_dim(by_half, core, axis=3, keepdims=False)
    send = lax.dynamic_index_in_dim(by_half, 1 - core, axis=3, keepdims=False)
    pair_sum = keep + lax.ppermute(send, "core", [(0, 1), (1, 0)])
    chunks = pair_sum.transpose(0, 2, 1, 3).reshape(plane_count, groups, half_width)
    reduced = jnp.sum(lax.all_to_all(chunks, "z", 0, 0, tiled=True), axis=0)
    bias = lax.dynamic_slice_in_dim(
        b_qkv.astype(jnp.float32), (seq_index % halves) * half_width, half_width
    )
    reduced = reduced + bias[None, :]
    owned_rows = lax.all_to_all(reduced, "tensor", 0, 0, tiled=True)
    gathered = lax.all_gather(owned_rows, SEQ, axis=0, tiled=False)
    combined_output = (
        gathered.reshape(steps, requests, halves, tensor_count, half_width)
        .transpose(0, 1, 3, 2, 4)
        .reshape(steps, requests, tensor_count * columns)
    )

    token_positions = (
        (prefix_lens[0] + suffix_lens)[None, :]
        + jnp.arange(steps, dtype=jnp.int32)[:, None]
    ).astype(jnp.float32)
    query_matrix = apply_rotary(
        combined_output[..., :query_width].reshape(steps, requests, QUERY_HEADS, HEAD_SIZE),
        token_positions,
    ).astype(jnp.bfloat16)
    keys_float = apply_rotary(
        combined_output[..., query_width : query_width + KEY_COLUMNS].reshape(
            steps, requests, KEY_HEADS, HEAD_SIZE
        ),
        token_positions,
    )
    values_float = combined_output[..., query_width + KEY_COLUMNS :].reshape(
        steps, requests, KEY_HEADS, HEAD_SIZE
    )
    current_keys = keys_float.astype(jnp.bfloat16)
    current_values = values_float.astype(jnp.bfloat16)
    new_keys = keys_float.reshape(steps, requests, KEY_COLUMNS).transpose(1, 0, 2)
    new_values = values_float.reshape(steps, requests, KEY_COLUMNS).transpose(1, 0, 2)
    query_by_group = (
        query_matrix.reshape(steps, requests, KEY_HEADS, query_group_width, HEAD_SIZE)
        .transpose(1, 2, 0, 3, 4)
        .reshape(requests, KEY_HEADS, query_rows, HEAD_SIZE)
    )

    prefix_key_block = prefix_key_cache[0].reshape(prefix_count, KEY_HEADS, HEAD_SIZE)
    prefix_value_block = prefix_value_cache[0].reshape(prefix_count, KEY_HEADS, HEAD_SIZE)
    suffix_key_block = suffix_key_cache.reshape(requests, suffix_count, KEY_HEADS, HEAD_SIZE)
    suffix_value_block = suffix_value_cache.reshape(requests, suffix_count, KEY_HEADS, HEAD_SIZE)
    score_pre = (
        jnp.einsum(
            "rhqd,phd->rhqp", query_by_group, prefix_key_block, preferred_element_type=jnp.float32
        )
        * scale
    )
    score_suf = (
        jnp.einsum(
            "rhqd,rshd->rhqs", query_by_group, suffix_key_block, preferred_element_type=jnp.float32
        )
        * scale
    )
    pre_mask = (
        seq_index * prefix_count + jnp.arange(prefix_count, dtype=jnp.int32) < prefix_lens[0]
    )[None, None, None, :]
    suf_mask = (
        (seq_index * suffix_count + jnp.arange(suffix_count, dtype=jnp.int32))[None, :]
        < suffix_lens[:, None]
    )[:, None, None, :]
    fill_pre = jnp.where(pre_mask, score_pre, masked_fill)
    fill_suf = jnp.where(suf_mask, score_suf, masked_fill)
    local_max = jnp.maximum(jnp.max(fill_pre, axis=3), jnp.max(fill_suf, axis=3))
    prob_pre = jnp.where(pre_mask, jnp.exp(fill_pre - local_max[..., None]), 0.0)
    prob_suf = jnp.where(suf_mask, jnp.exp(fill_suf - local_max[..., None]), 0.0)
    local_weight = jnp.sum(prob_pre, axis=3) + jnp.sum(prob_suf, axis=3)
    local_acc = jnp.einsum(
        "rhqp,phd->rhqd",
        prob_pre.astype(jnp.bfloat16),
        prefix_value_block,
        preferred_element_type=jnp.float32,
    )
    local_acc = local_acc + jnp.einsum(
        "rhqs,rshd->rhqd",
        prob_suf.astype(jnp.bfloat16),
        suffix_value_block,
        preferred_element_type=jnp.float32,
    )

    fresh_k = current_keys.transpose(1, 2, 0, 3)
    fresh_v = current_values.transpose(1, 2, 0, 3)
    score_new = (
        jnp.einsum("rhqd,rhid->rhqi", query_by_group, fresh_k, preferred_element_type=jnp.float32)
        * scale
    )
    new_mask = (
        (jnp.arange(query_rows, dtype=jnp.int32) // query_group_width)[:, None]
        >= jnp.arange(steps, dtype=jnp.int32)[None, :]
    )[None, None]
    fill_new = jnp.where(new_mask, score_new, masked_fill)
    new_max = jnp.max(fill_new, axis=3)
    prob_new = jnp.where(new_mask, jnp.exp(fill_new - new_max[..., None]), 0.0)
    new_weight = jnp.sum(prob_new, axis=3)
    new_acc = jnp.einsum(
        "rhqi,rhid->rhqd",
        prob_new.astype(jnp.bfloat16),
        fresh_v,
        preferred_element_type=jnp.float32,
    )

    lane_pad = ((0, 0), (0, 0), (0, HEAD_SIZE - query_rows))
    packed = jnp.concatenate(
        [
            local_acc,
            jnp.pad(local_max, lane_pad)[:, :, None, :],
            jnp.pad(local_weight, lane_pad)[:, :, None, :],
        ],
        axis=2,
    ).reshape(requests, KEY_HEADS // 2, 2, query_rows + 2, HEAD_SIZE)
    keep = lax.dynamic_index_in_dim(packed, core, axis=2, keepdims=False)
    came = lax.ppermute(
        lax.dynamic_index_in_dim(packed, 1 - core, axis=2, keepdims=False), "core", [(0, 1), (1, 0)]
    )
    keep_max = keep[..., query_rows, :query_rows]
    came_max = came[..., query_rows, :query_rows]
    pair_max = jnp.maximum(keep_max, came_max)
    keep_factor = jnp.exp(keep_max - pair_max)
    came_factor = jnp.exp(came_max - pair_max)
    pair_weight = (
        keep[..., query_rows + 1, :query_rows] * keep_factor
        + came[..., query_rows + 1, :query_rows] * came_factor
    )
    pair_acc = (
        keep[..., :query_rows, :] * keep_factor[..., None]
        + came[..., :query_rows, :] * came_factor[..., None]
    )
    pad_rows = ((0, 0), (0, 0), (0, HEAD_SIZE - query_rows))
    pair_packed = jnp.concatenate(
        [
            pair_acc,
            jnp.pad(pair_max, pad_rows)[:, :, None, :],
            jnp.pad(pair_weight, pad_rows)[:, :, None, :],
        ],
        axis=2,
    ).reshape(seq_count // 2, query_rows + 2, HEAD_SIZE)
    arrived = lax.all_to_all(pair_packed, "z", 0, 0, tiled=True)
    w_out_cols, arrived = lax.optimization_barrier((w_out_cols, arrived))
    part_acc = arrived[:, :query_rows, :]
    part_max = arrived[:, query_rows, :query_rows]
    part_weight = arrived[:, query_rows + 1, :query_rows]
    global_max = jnp.max(part_max, axis=0)
    factor = jnp.exp(part_max - global_max[None])
    global_weight = jnp.sum(part_weight * factor, axis=0)
    global_acc = jnp.sum(part_acc * factor[..., None], axis=0)

    mine_r = seq_index // KEY_HEADS
    mine_h = seq_index % KEY_HEADS
    own_new_max = new_max[mine_r, mine_h]
    own_new_weight = new_weight[mine_r, mine_h]
    own_new_acc = new_acc[mine_r, mine_h]
    top = jnp.maximum(global_max, own_new_max)
    factor_old = jnp.exp(global_max - top)
    factor_new = jnp.exp(own_new_max - top)
    total = global_weight * factor_old + own_new_weight * factor_new
    summed = global_acc * factor_old[..., None] + own_new_acc * factor_new[..., None]
    attention_slice = (summed / total[..., None]).astype(jnp.bfloat16)

    attention_all = lax.all_to_all(
        jnp.broadcast_to(attention_slice[None], (seq_count,) + attention_slice.shape),
        SEQ, 0, 0, tiled=True,
    )
    heads_local = (
        attention_all.reshape(requests, KEY_HEADS, steps, query_group_width, HEAD_SIZE)
        .transpose(2, 0, 1, 3, 4)
        .reshape(steps, requests, query_width)
    )
    owned = jnp.einsum("sbc,cd->sbd", heads_local, w_out_cols, preferred_element_type=jnp.float32)
    return (owned, new_keys, new_values)


def solution(mesh):
    placed = (
        P(None, None, SEQ),
        P(SEQ),
        P(SEQ, "tensor"),
        P("tensor"),
        P("tensor", SEQ),
        P("tensor", SEQ, None),
        P("tensor", SEQ, None),
        P("tensor", SEQ, None),
        P("tensor", SEQ, None),
        P("tensor"),
        P("tensor"),
    )
    planes = jax.sharding.Mesh(
        mesh.devices.reshape(-1, 2, mesh.devices.shape[1]), ("z", "core", "tensor")
    )
    return jax.shard_map(
        body,
        mesh=planes,
        in_specs=placed,
        out_specs=(P(None, "tensor", ("z", "core")), P("tensor", None, None), P("tensor", None, None)),
        check_vma=False,
    )
```

```python
import jax
import jax.numpy as jnp
from jax import lax
from jax.sharding import PartitionSpec as P

D = 5120
QUERY_HEADS = 40
KEY_HEADS = 8
HEAD_SIZE = 128
KEY_COLUMNS = 1024


SEQ = ("z", "core")
epsilon = 1e-06
masked_fill = -1e30


def apply_rotary(values, token_positions):
    half = values.shape[-1] // 2
    freq = jnp.exp(
        -(jnp.arange(half, dtype=jnp.float32) * (2.0 / values.shape[-1]))
        * jnp.log(jnp.float32(1000000.0))
    )
    angles = token_positions[..., None, None] * freq
    cosine = jnp.cos(angles)
    sine = jnp.sin(angles)
    left = values[..., :half]
    right = values[..., half:]
    return jnp.concatenate([left * cosine - right * sine, right * cosine + left * sine], axis=-1)


def body(
    hidden,
    norm_gain,
    w_qkv,
    b_qkv,
    w_out,
    prefix_key_cache,
    prefix_value_cache,
    suffix_key_cache,
    suffix_value_cache,
    prefix_lens,
    suffix_lens,
):
    seq_count = lax.axis_size(SEQ)
    tensor_count = lax.axis_size("tensor")
    steps = hidden.shape[0]
    request_total = hidden.shape[1]
    requests = suffix_lens.shape[0]
    columns = w_qkv.shape[1]
    prefix_count = prefix_key_cache.shape[1]
    suffix_count = suffix_key_cache.shape[1]
    query_group_width = QUERY_HEADS // KEY_HEADS
    query_width = QUERY_HEADS * HEAD_SIZE
    query_rows = steps * query_group_width
    scale = float(HEAD_SIZE) ** (-0.5)
    seq_index = lax.axis_index(SEQ)

    w_out_cols = lax.all_gather(w_out, "tensor", axis=0, tiled=True)

    xf = hidden.astype(jnp.float32)
    local_squares = jnp.sum(xf * xf, axis=2)
    squares = jnp.sum(
        lax.all_to_all(
            jnp.broadcast_to(local_squares[None], (seq_count,) + local_squares.shape),
            SEQ, 0, 0, tiled=True,
        ),
        axis=0,
    )
    normed = (
        xf * lax.rsqrt(squares / D + epsilon)[..., None] * norm_gain.astype(jnp.float32)
    ).astype(jnp.bfloat16)
    partial_value = jnp.einsum("sbd,dc->sbc", normed, w_qkv, preferred_element_type=jnp.float32)

    halves = seq_count // (steps * requests)
    half_width = columns // halves
    groups = request_total // requests
    core = lax.axis_index("core")
    plane_count = seq_count // halves
    by_half = partial_value.reshape(steps, groups, requests, halves, half_width)
    keep = lax.dynamic_index_in_dim(by_half, core, axis=3, keepdims=False)
    send = lax.dynamic_index_in_dim(by_half, 1 - core, axis=3, keepdims=False)
    pair_sum = keep + lax.ppermute(send, "core", [(0, 1), (1, 0)])
    chunks = pair_sum.transpose(0, 2, 1, 3).reshape(plane_count, groups, half_width)
    reduced = jnp.sum(lax.all_to_all(chunks, "z", 0, 0, tiled=True), axis=0)
    bias = lax.dynamic_slice_in_dim(
        b_qkv.astype(jnp.float32), (seq_index % halves) * half_width, half_width
    )
    reduced = reduced + bias[None, :]
    owned_rows = lax.all_to_all(reduced, "tensor", 0, 0, tiled=True)
    gathered = lax.all_to_all(
        jnp.broadcast_to(owned_rows[None], (seq_count,) + owned_rows.shape), SEQ, 0, 0, tiled=True
    )
    combined_output = (
        gathered.reshape(steps, requests, halves, tensor_count, half_width)
        .transpose(0, 1, 3, 2, 4)
        .reshape(steps, requests, tensor_count * columns)
    )

    token_positions = (
        (prefix_lens[0] + suffix_lens)[None, :]
        + jnp.arange(steps, dtype=jnp.int32)[:, None]
    ).astype(jnp.float32)
    query_matrix = apply_rotary(
        combined_output[..., :query_width].reshape(steps, requests, QUERY_HEADS, HEAD_SIZE),
        token_positions,
    ).astype(jnp.bfloat16)
    keys_float = apply_rotary(
        combined_output[..., query_width : query_width + KEY_COLUMNS].reshape(
            steps, requests, KEY_HEADS, HEAD_SIZE
        ),
        token_positions,
    )
    values_float = combined_output[..., query_width + KEY_COLUMNS :].reshape(
        steps, requests, KEY_HEADS, HEAD_SIZE
    )
    current_keys = keys_float.astype(jnp.bfloat16)
    current_values = values_float.astype(jnp.bfloat16)
    new_keys = keys_float.reshape(steps, requests, KEY_COLUMNS).transpose(1, 0, 2)
    new_values = values_float.reshape(steps, requests, KEY_COLUMNS).transpose(1, 0, 2)
    query_by_group = (
        query_matrix.reshape(steps, requests, KEY_HEADS, query_group_width, HEAD_SIZE)
        .transpose(1, 2, 0, 3, 4)
        .reshape(requests, KEY_HEADS, query_rows, HEAD_SIZE)
    )

    prefix_key_block = prefix_key_cache[0].reshape(prefix_count, KEY_HEADS, HEAD_SIZE)
    prefix_value_block = prefix_value_cache[0].reshape(prefix_count, KEY_HEADS, HEAD_SIZE)
    suffix_key_block = suffix_key_cache.reshape(requests, suffix_count, KEY_HEADS, HEAD_SIZE)
    suffix_value_block = suffix_value_cache.reshape(requests, suffix_count, KEY_HEADS, HEAD_SIZE)
    score_pre = (
        jnp.einsum(
            "rhqd,phd->rhqp", query_by_group, prefix_key_block, preferred_element_type=jnp.float32
        )
        * scale
    )
    score_suf = (
        jnp.einsum(
            "rhqd,rshd->rhqs", query_by_group, suffix_key_block, preferred_element_type=jnp.float32
        )
        * scale
    )
    pre_mask = (
        seq_index * prefix_count + jnp.arange(prefix_count, dtype=jnp.int32) < prefix_lens[0]
    )[None, None, None, :]
    suf_mask = (
        (seq_index * suffix_count + jnp.arange(suffix_count, dtype=jnp.int32))[None, :]
        < suffix_lens[:, None]
    )[:, None, None, :]
    fill_pre = jnp.where(pre_mask, score_pre, masked_fill)
    fill_suf = jnp.where(suf_mask, score_suf, masked_fill)
    local_max = jnp.maximum(jnp.max(fill_pre, axis=3), jnp.max(fill_suf, axis=3))
    prob_pre = jnp.where(pre_mask, jnp.exp(fill_pre - local_max[..., None]), 0.0)
    prob_suf = jnp.where(suf_mask, jnp.exp(fill_suf - local_max[..., None]), 0.0)
    local_weight = jnp.sum(prob_pre, axis=3) + jnp.sum(prob_suf, axis=3)
    local_acc = jnp.einsum(
        "rhqp,phd->rhqd",
        prob_pre.astype(jnp.bfloat16),
        prefix_value_block,
        preferred_element_type=jnp.float32,
    )
    local_acc = local_acc + jnp.einsum(
        "rhqs,rshd->rhqd",
        prob_suf.astype(jnp.bfloat16),
        suffix_value_block,
        preferred_element_type=jnp.float32,
    )

    fresh_k = current_keys.transpose(1, 2, 0, 3)
    fresh_v = current_values.transpose(1, 2, 0, 3)
    score_new = (
        jnp.einsum("rhqd,rhid->rhqi", query_by_group, fresh_k, preferred_element_type=jnp.float32)
        * scale
    )
    new_mask = (
        (jnp.arange(query_rows, dtype=jnp.int32) // query_group_width)[:, None]
        >= jnp.arange(steps, dtype=jnp.int32)[None, :]
    )[None, None]
    fill_new = jnp.where(new_mask, score_new, masked_fill)
    new_max = jnp.max(fill_new, axis=3)
    prob_new = jnp.where(new_mask, jnp.exp(fill_new - new_max[..., None]), 0.0)
    new_weight = jnp.sum(prob_new, axis=3)
    new_acc = jnp.einsum(
        "rhqi,rhid->rhqd",
        prob_new.astype(jnp.bfloat16),
        fresh_v,
        preferred_element_type=jnp.float32,
    )

    lane_pad = ((0, 0), (0, 0), (0, HEAD_SIZE - query_rows))
    packed = jnp.concatenate(
        [
            local_acc,
            jnp.pad(local_max, lane_pad)[:, :, None, :],
            jnp.pad(local_weight, lane_pad)[:, :, None, :],
        ],
        axis=2,
    ).reshape(requests, KEY_HEADS // 2, 2, query_rows + 2, HEAD_SIZE)
    keep = lax.dynamic_index_in_dim(packed, core, axis=2, keepdims=False)
    came = lax.ppermute(
        lax.dynamic_index_in_dim(packed, 1 - core, axis=2, keepdims=False), "core", [(0, 1), (1, 0)]
    )
    keep_max = keep[..., query_rows, :query_rows]
    came_max = came[..., query_rows, :query_rows]
    pair_max = jnp.maximum(keep_max, came_max)
    keep_factor = jnp.exp(keep_max - pair_max)
    came_factor = jnp.exp(came_max - pair_max)
    pair_weight = (
        keep[..., query_rows + 1, :query_rows] * keep_factor
        + came[..., query_rows + 1, :query_rows] * came_factor
    )
    pair_acc = (
        keep[..., :query_rows, :] * keep_factor[..., None]
        + came[..., :query_rows, :] * came_factor[..., None]
    )
    pad_rows = ((0, 0), (0, 0), (0, HEAD_SIZE - query_rows))
    pair_packed = jnp.concatenate(
        [
            pair_acc,
            jnp.pad(pair_max, pad_rows)[:, :, None, :],
            jnp.pad(pair_weight, pad_rows)[:, :, None, :],
        ],
        axis=2,
    ).reshape(seq_count // 2, query_rows + 2, HEAD_SIZE)
    arrived = lax.all_to_all(pair_packed, "z", 0, 0, tiled=True)
    w_out_cols, arrived = lax.optimization_barrier((w_out_cols, arrived))
    part_acc = arrived[:, :query_rows, :]
    part_max = arrived[:, query_rows, :query_rows]
    part_weight = arrived[:, query_rows + 1, :query_rows]
    global_max = jnp.max(part_max, axis=0)
    factor = jnp.exp(part_max - global_max[None])
    global_weight = jnp.sum(part_weight * factor, axis=0)
    global_acc = jnp.sum(part_acc * factor[..., None], axis=0)

    mine_r = seq_index // KEY_HEADS
    mine_h = seq_index % KEY_HEADS
    own_new_max = new_max[mine_r, mine_h]
    own_new_weight = new_weight[mine_r, mine_h]
    own_new_acc = new_acc[mine_r, mine_h]
    top = jnp.maximum(global_max, own_new_max)
    factor_old = jnp.exp(global_max - top)
    factor_new = jnp.exp(own_new_max - top)
    total = global_weight * factor_old + own_new_weight * factor_new
    summed = global_acc * factor_old[..., None] + own_new_acc * factor_new[..., None]
    attention_slice = (summed / total[..., None]).astype(jnp.bfloat16)

    attention_all = lax.all_to_all(
        jnp.broadcast_to(attention_slice[None], (seq_count,) + attention_slice.shape),
        SEQ, 0, 0, tiled=True,
    )
    heads_local = (
        attention_all.reshape(requests, KEY_HEADS, steps, query_group_width, HEAD_SIZE)
        .transpose(2, 0, 1, 3, 4)
        .reshape(steps, requests, query_width)
    )
    owned = jnp.einsum("sbc,cd->sbd", heads_local, w_out_cols, preferred_element_type=jnp.float32)
    return (owned, new_keys, new_values)


def solution(mesh):
    placed = (
        P(None, None, SEQ),
        P(SEQ),
        P(SEQ, "tensor"),
        P("tensor"),
        P("tensor", SEQ),
        P("tensor", SEQ, None),
        P("tensor", SEQ, None),
        P("tensor", SEQ, None),
        P("tensor", SEQ, None),
        P("tensor"),
        P("tensor"),
    )
    planes = jax.sharding.Mesh(
        mesh.devices.reshape(-1, 2, mesh.devices.shape[1]), ("z", "core", "tensor")
    )
    return jax.shard_map(
        body,
        mesh=planes,
        in_specs=placed,
        out_specs=(P(None, "tensor", ("z", "core")), P("tensor", None, None), P("tensor", None, None)),
        check_vma=False,
    )
```

```python
import jax
import jax.numpy as jnp
from jax import lax
from jax.sharding import PartitionSpec as P

D = 5120
QUERY_HEADS = 40
KEY_HEADS = 8
HEAD_SIZE = 128
KEY_COLUMNS = 1024


SEQ = ("z", "core")
epsilon = 1e-06
masked_fill = -1e30


def apply_rotary(values, token_positions):
    half = values.shape[-1] // 2
    freq = jnp.exp(
        -(jnp.arange(half, dtype=jnp.float32) * (2.0 / values.shape[-1]))
        * jnp.log(jnp.float32(1000000.0))
    )
    angles = token_positions[..., None, None] * freq
    cosine = jnp.cos(angles)
    sine = jnp.sin(angles)
    left = values[..., :half]
    right = values[..., half:]
    return jnp.concatenate([left * cosine - right * sine, right * cosine + left * sine], axis=-1)


def body(
    hidden,
    norm_gain,
    w_qkv,
    b_qkv,
    w_out,
    prefix_key_cache,
    prefix_value_cache,
    suffix_key_cache,
    suffix_value_cache,
    prefix_lens,
    suffix_lens,
):
    seq_count = lax.axis_size(SEQ)
    tensor_count = lax.axis_size("tensor")
    steps = hidden.shape[0]
    request_total = hidden.shape[1]
    requests = suffix_lens.shape[0]
    columns = w_qkv.shape[1]
    prefix_count = prefix_key_cache.shape[1]
    suffix_count = suffix_key_cache.shape[1]
    query_group_width = QUERY_HEADS // KEY_HEADS
    query_width = QUERY_HEADS * HEAD_SIZE
    query_rows = steps * query_group_width
    scale = float(HEAD_SIZE) ** (-0.5)
    seq_index = lax.axis_index(SEQ)

    w_out_cols = lax.all_to_all(
        jnp.broadcast_to(w_out[None], (tensor_count,) + w_out.shape), "tensor", 0, 0, tiled=True
    ).reshape(-1, w_out.shape[1])

    xf = hidden.astype(jnp.float32)
    local_squares = jnp.sum(xf * xf, axis=2)
    squares = jnp.sum(
        lax.all_to_all(
            jnp.broadcast_to(local_squares[None], (seq_count,) + local_squares.shape),
            SEQ, 0, 0, tiled=True,
        ),
        axis=0,
    )
    normed = (
        xf * lax.rsqrt(squares / D + epsilon)[..., None] * norm_gain.astype(jnp.float32)
    ).astype(jnp.bfloat16)
    partial_value = jnp.einsum("sbd,dc->sbc", normed, w_qkv, preferred_element_type=jnp.float32)

    halves = seq_count // (steps * requests)
    half_width = columns // halves
    groups = request_total // requests
    core = lax.axis_index("core")
    plane_count = seq_count // halves
    by_half = partial_value.reshape(steps, groups, requests, halves, half_width)
    keep = lax.dynamic_index_in_dim(by_half, core, axis=3, keepdims=False)
    send = lax.dynamic_index_in_dim(by_half, 1 - core, axis=3, keepdims=False)
    pair_sum = keep + lax.ppermute(send, "core", [(0, 1), (1, 0)])
    chunks = pair_sum.transpose(0, 2, 1, 3).reshape(plane_count, groups, half_width)
    reduced = jnp.sum(lax.all_to_all(chunks, "z", 0, 0, tiled=True), axis=0)
    bias = lax.dynamic_slice_in_dim(
        b_qkv.astype(jnp.float32), (seq_index % halves) * half_width, half_width
    )
    reduced = reduced + bias[None, :]
    owned_rows = lax.all_to_all(reduced, "tensor", 0, 0, tiled=True)
    gathered = lax.all_gather(owned_rows, SEQ, axis=0, tiled=False)
    combined_output = (
        gathered.reshape(steps, requests, halves, tensor_count, half_width)
        .transpose(0, 1, 3, 2, 4)
        .reshape(steps, requests, tensor_count * columns)
    )

    token_positions = (
        (prefix_lens[0] + suffix_lens)[None, :]
        + jnp.arange(steps, dtype=jnp.int32)[:, None]
    ).astype(jnp.float32)
    query_matrix = apply_rotary(
        combined_output[..., :query_width].reshape(steps, requests, QUERY_HEADS, HEAD_SIZE),
        token_positions,
    ).astype(jnp.bfloat16)
    keys_float = apply_rotary(
        combined_output[..., query_width : query_width + KEY_COLUMNS].reshape(
            steps, requests, KEY_HEADS, HEAD_SIZE
        ),
        token_positions,
    )
    values_float = combined_output[..., query_width + KEY_COLUMNS :].reshape(
        steps, requests, KEY_HEADS, HEAD_SIZE
    )
    current_keys = keys_float.astype(jnp.bfloat16)
    current_values = values_float.astype(jnp.bfloat16)
    new_keys = keys_float.reshape(steps, requests, KEY_COLUMNS).transpose(1, 0, 2)
    new_values = values_float.reshape(steps, requests, KEY_COLUMNS).transpose(1, 0, 2)
    query_by_group = (
        query_matrix.reshape(steps, requests, KEY_HEADS, query_group_width, HEAD_SIZE)
        .transpose(1, 2, 0, 3, 4)
        .reshape(requests, KEY_HEADS, query_rows, HEAD_SIZE)
    )

    prefix_key_block = prefix_key_cache[0].reshape(prefix_count, KEY_HEADS, HEAD_SIZE)
    prefix_value_block = prefix_value_cache[0].reshape(prefix_count, KEY_HEADS, HEAD_SIZE)
    suffix_key_block = suffix_key_cache.reshape(requests, suffix_count, KEY_HEADS, HEAD_SIZE)
    suffix_value_block = suffix_value_cache.reshape(requests, suffix_count, KEY_HEADS, HEAD_SIZE)
    score_pre = (
        jnp.einsum(
            "rhqd,phd->rhqp", query_by_group, prefix_key_block, preferred_element_type=jnp.float32
        )
        * scale
    )
    score_suf = (
        jnp.einsum(
            "rhqd,rshd->rhqs", query_by_group, suffix_key_block, preferred_element_type=jnp.float32
        )
        * scale
    )
    pre_mask = (
        seq_index * prefix_count + jnp.arange(prefix_count, dtype=jnp.int32) < prefix_lens[0]
    )[None, None, None, :]
    suf_mask = (
        (seq_index * suffix_count + jnp.arange(suffix_count, dtype=jnp.int32))[None, :]
        < suffix_lens[:, None]
    )[:, None, None, :]
    fill_pre = jnp.where(pre_mask, score_pre, masked_fill)
    fill_suf = jnp.where(suf_mask, score_suf, masked_fill)
    local_max = jnp.maximum(jnp.max(fill_pre, axis=3), jnp.max(fill_suf, axis=3))
    prob_pre = jnp.where(pre_mask, jnp.exp(fill_pre - local_max[..., None]), 0.0)
    prob_suf = jnp.where(suf_mask, jnp.exp(fill_suf - local_max[..., None]), 0.0)
    local_weight = jnp.sum(prob_pre, axis=3) + jnp.sum(prob_suf, axis=3)
    local_acc = jnp.einsum(
        "rhqp,phd->rhqd",
        prob_pre.astype(jnp.bfloat16),
        prefix_value_block,
        preferred_element_type=jnp.float32,
    )
    local_acc = local_acc + jnp.einsum(
        "rhqs,rshd->rhqd",
        prob_suf.astype(jnp.bfloat16),
        suffix_value_block,
        preferred_element_type=jnp.float32,
    )

    fresh_k = current_keys.transpose(1, 2, 0, 3)
    fresh_v = current_values.transpose(1, 2, 0, 3)
    score_new = (
        jnp.einsum("rhqd,rhid->rhqi", query_by_group, fresh_k, preferred_element_type=jnp.float32)
        * scale
    )
    new_mask = (
        (jnp.arange(query_rows, dtype=jnp.int32) // query_group_width)[:, None]
        >= jnp.arange(steps, dtype=jnp.int32)[None, :]
    )[None, None]
    fill_new = jnp.where(new_mask, score_new, masked_fill)
    new_max = jnp.max(fill_new, axis=3)
    prob_new = jnp.where(new_mask, jnp.exp(fill_new - new_max[..., None]), 0.0)
    new_weight = jnp.sum(prob_new, axis=3)
    new_acc = jnp.einsum(
        "rhqi,rhid->rhqd",
        prob_new.astype(jnp.bfloat16),
        fresh_v,
        preferred_element_type=jnp.float32,
    )

    lane_pad = ((0, 0), (0, 0), (0, HEAD_SIZE - query_rows))
    packed = jnp.concatenate(
        [
            local_acc,
            jnp.pad(local_max, lane_pad)[:, :, None, :],
            jnp.pad(local_weight, lane_pad)[:, :, None, :],
        ],
        axis=2,
    ).reshape(requests, KEY_HEADS // 2, 2, query_rows + 2, HEAD_SIZE)
    keep = lax.dynamic_index_in_dim(packed, core, axis=2, keepdims=False)
    came = lax.ppermute(
        lax.dynamic_index_in_dim(packed, 1 - core, axis=2, keepdims=False), "core", [(0, 1), (1, 0)]
    )
    keep_max = keep[..., query_rows, :query_rows]
    came_max = came[..., query_rows, :query_rows]
    pair_max = jnp.maximum(keep_max, came_max)
    keep_factor = jnp.exp(keep_max - pair_max)
    came_factor = jnp.exp(came_max - pair_max)
    pair_weight = (
        keep[..., query_rows + 1, :query_rows] * keep_factor
        + came[..., query_rows + 1, :query_rows] * came_factor
    )
    pair_acc = (
        keep[..., :query_rows, :] * keep_factor[..., None]
        + came[..., :query_rows, :] * came_factor[..., None]
    )
    pad_rows = ((0, 0), (0, 0), (0, HEAD_SIZE - query_rows))
    pair_packed = jnp.concatenate(
        [
            pair_acc,
            jnp.pad(pair_max, pad_rows)[:, :, None, :],
            jnp.pad(pair_weight, pad_rows)[:, :, None, :],
        ],
        axis=2,
    ).reshape(seq_count // 2, query_rows + 2, HEAD_SIZE)
    arrived = lax.all_to_all(pair_packed, "z", 0, 0, tiled=True)
    w_out_cols, arrived = lax.optimization_barrier((w_out_cols, arrived))
    part_acc = arrived[:, :query_rows, :]
    part_max = arrived[:, query_rows, :query_rows]
    part_weight = arrived[:, query_rows + 1, :query_rows]
    global_max = jnp.max(part_max, axis=0)
    factor = jnp.exp(part_max - global_max[None])
    global_weight = jnp.sum(part_weight * factor, axis=0)
    global_acc = jnp.sum(part_acc * factor[..., None], axis=0)

    mine_r = seq_index // KEY_HEADS
    mine_h = seq_index % KEY_HEADS
    own_new_max = new_max[mine_r, mine_h]
    own_new_weight = new_weight[mine_r, mine_h]
    own_new_acc = new_acc[mine_r, mine_h]
    top = jnp.maximum(global_max, own_new_max)
    factor_old = jnp.exp(global_max - top)
    factor_new = jnp.exp(own_new_max - top)
    total = global_weight * factor_old + own_new_weight * factor_new
    summed = global_acc * factor_old[..., None] + own_new_acc * factor_new[..., None]
    attention_slice = (summed / total[..., None]).astype(jnp.bfloat16)

    attention_all = lax.all_to_all(
        jnp.broadcast_to(attention_slice[None], (seq_count,) + attention_slice.shape),
        SEQ, 0, 0, tiled=True,
    )
    heads_local = (
        attention_all.reshape(requests, KEY_HEADS, steps, query_group_width, HEAD_SIZE)
        .transpose(2, 0, 1, 3, 4)
        .reshape(steps, requests, query_width)
    )
    owned = jnp.einsum("sbc,cd->sbd", heads_local, w_out_cols, preferred_element_type=jnp.float32)
    return (owned, new_keys, new_values)


def solution(mesh):
    placed = (
        P(None, None, SEQ),
        P(SEQ),
        P(SEQ, "tensor"),
        P("tensor"),
        P("tensor", SEQ),
        P("tensor", SEQ, None),
        P("tensor", SEQ, None),
        P("tensor", SEQ, None),
        P("tensor", SEQ, None),
        P("tensor"),
        P("tensor"),
    )
    planes = jax.sharding.Mesh(
        mesh.devices.reshape(-1, 2, mesh.devices.shape[1]), ("z", "core", "tensor")
    )
    return jax.shard_map(
        body,
        mesh=planes,
        in_specs=placed,
        out_specs=(P(None, "tensor", ("z", "core")), P("tensor", None, None), P("tensor", None, None)),
        check_vma=False,
    )
```

```python
import jax
import jax.numpy as jnp
from jax import lax
from jax.sharding import PartitionSpec as P

D = 5120
QUERY_HEADS = 40
KEY_HEADS = 8
HEAD_SIZE = 128
KEY_COLUMNS = 1024


SEQ = ("z", "core")
epsilon = 1e-06
masked_fill = -1e30


def apply_rotary(values, token_positions):
    half = values.shape[-1] // 2
    freq = jnp.exp(
        -(jnp.arange(half, dtype=jnp.float32) * (2.0 / values.shape[-1]))
        * jnp.log(jnp.float32(1000000.0))
    )
    angles = token_positions[..., None, None] * freq
    cosine = jnp.cos(angles)
    sine = jnp.sin(angles)
    left = values[..., :half]
    right = values[..., half:]
    return jnp.concatenate([left * cosine - right * sine, right * cosine + left * sine], axis=-1)


def body(
    hidden,
    norm_gain,
    w_qkv,
    b_qkv,
    w_out,
    prefix_key_cache,
    prefix_value_cache,
    suffix_key_cache,
    suffix_value_cache,
    prefix_lens,
    suffix_lens,
):
    seq_count = lax.axis_size(SEQ)
    tensor_count = lax.axis_size("tensor")
    steps = hidden.shape[0]
    request_total = hidden.shape[1]
    requests = suffix_lens.shape[0]
    columns = w_qkv.shape[1]
    prefix_count = prefix_key_cache.shape[1]
    suffix_count = suffix_key_cache.shape[1]
    query_group_width = QUERY_HEADS // KEY_HEADS
    query_width = QUERY_HEADS * HEAD_SIZE
    query_rows = steps * query_group_width
    scale = float(HEAD_SIZE) ** (-0.5)
    seq_index = lax.axis_index(SEQ)

    w_out_rows = lax.all_to_all(
        jnp.broadcast_to(w_out[None], (tensor_count,) + w_out.shape), "tensor", 0, 0, tiled=True
    )

    xf = hidden.astype(jnp.float32)
    local_squares = jnp.sum(xf * xf, axis=2)
    squares = jnp.sum(
        lax.all_to_all(
            jnp.broadcast_to(local_squares[None], (seq_count,) + local_squares.shape),
            SEQ, 0, 0, tiled=True,
        ),
        axis=0,
    )
    normed = (
        xf * lax.rsqrt(squares / D + epsilon)[..., None] * norm_gain.astype(jnp.float32)
    ).astype(jnp.bfloat16)
    partial_value = jnp.einsum("sbd,dc->sbc", normed, w_qkv, preferred_element_type=jnp.float32)

    halves = seq_count // (steps * requests)
    half_width = columns // halves
    groups = request_total // requests
    core = lax.axis_index("core")
    plane_count = seq_count // halves
    by_half = partial_value.reshape(steps, groups, requests, halves, half_width)
    keep = lax.dynamic_index_in_dim(by_half, core, axis=3, keepdims=False)
    send = lax.dynamic_index_in_dim(by_half, 1 - core, axis=3, keepdims=False)
    pair_sum = keep + lax.ppermute(send, "core", [(0, 1), (1, 0)])
    chunks = pair_sum.transpose(0, 2, 1, 3).reshape(plane_count, groups, half_width)
    reduced = jnp.sum(lax.all_to_all(chunks, "z", 0, 0, tiled=True), axis=0)
    bias = lax.dynamic_slice_in_dim(
        b_qkv.astype(jnp.float32), (seq_index % halves) * half_width, half_width
    )
    reduced = reduced + bias[None, :]
    owned_rows = lax.all_to_all(reduced, "tensor", 0, 0, tiled=True)
    gathered = lax.all_gather(owned_rows, SEQ, axis=0, tiled=False)
    combined_output = (
        gathered.reshape(steps, requests, halves, tensor_count, half_width)
        .transpose(0, 1, 3, 2, 4)
        .reshape(steps, requests, tensor_count * columns)
    )

    token_positions = (
        (prefix_lens[0] + suffix_lens)[None, :]
        + jnp.arange(steps, dtype=jnp.int32)[:, None]
    ).astype(jnp.float32)
    query_matrix = apply_rotary(
        combined_output[..., :query_width].reshape(steps, requests, QUERY_HEADS, HEAD_SIZE),
        token_positions,
    ).astype(jnp.bfloat16)
    keys_float = apply_rotary(
        combined_output[..., query_width : query_width + KEY_COLUMNS].reshape(
            steps, requests, KEY_HEADS, HEAD_SIZE
        ),
        token_positions,
    )
    values_float = combined_output[..., query_width + KEY_COLUMNS :].reshape(
        steps, requests, KEY_HEADS, HEAD_SIZE
    )
    current_keys = keys_float.astype(jnp.bfloat16)
    current_values = values_float.astype(jnp.bfloat16)
    new_keys = keys_float.reshape(steps, requests, KEY_COLUMNS).transpose(1, 0, 2)
    new_values = values_float.reshape(steps, requests, KEY_COLUMNS).transpose(1, 0, 2)
    query_by_group = (
        query_matrix.reshape(steps, requests, KEY_HEADS, query_group_width, HEAD_SIZE)
        .transpose(1, 2, 0, 3, 4)
        .reshape(requests, KEY_HEADS, query_rows, HEAD_SIZE)
    )
    w_out_rows, query_by_group = lax.optimization_barrier((w_out_rows, query_by_group))
    w_out_cols = w_out_rows.reshape(-1, w_out.shape[1])

    prefix_key_block = prefix_key_cache[0].reshape(prefix_count, KEY_HEADS, HEAD_SIZE)
    prefix_value_block = prefix_value_cache[0].reshape(prefix_count, KEY_HEADS, HEAD_SIZE)
    suffix_key_block = suffix_key_cache.reshape(requests, suffix_count, KEY_HEADS, HEAD_SIZE)
    suffix_value_block = suffix_value_cache.reshape(requests, suffix_count, KEY_HEADS, HEAD_SIZE)
    score_pre = (
        jnp.einsum(
            "rhqd,phd->rhqp", query_by_group, prefix_key_block, preferred_element_type=jnp.float32
        )
        * scale
    )
    score_suf = (
        jnp.einsum(
            "rhqd,rshd->rhqs", query_by_group, suffix_key_block, preferred_element_type=jnp.float32
        )
        * scale
    )
    pre_mask = (
        seq_index * prefix_count + jnp.arange(prefix_count, dtype=jnp.int32) < prefix_lens[0]
    )[None, None, None, :]
    suf_mask = (
        (seq_index * suffix_count + jnp.arange(suffix_count, dtype=jnp.int32))[None, :]
        < suffix_lens[:, None]
    )[:, None, None, :]
    fill_pre = jnp.where(pre_mask, score_pre, masked_fill)
    fill_suf = jnp.where(suf_mask, score_suf, masked_fill)
    local_max = jnp.maximum(jnp.max(fill_pre, axis=3), jnp.max(fill_suf, axis=3))
    prob_pre = jnp.where(pre_mask, jnp.exp(fill_pre - local_max[..., None]), 0.0)
    prob_suf = jnp.where(suf_mask, jnp.exp(fill_suf - local_max[..., None]), 0.0)
    local_weight = jnp.sum(prob_pre, axis=3) + jnp.sum(prob_suf, axis=3)
    local_acc = jnp.einsum(
        "rhqp,phd->rhqd",
        prob_pre.astype(jnp.bfloat16),
        prefix_value_block,
        preferred_element_type=jnp.float32,
    )
    local_acc = local_acc + jnp.einsum(
        "rhqs,rshd->rhqd",
        prob_suf.astype(jnp.bfloat16),
        suffix_value_block,
        preferred_element_type=jnp.float32,
    )

    fresh_k = current_keys.transpose(1, 2, 0, 3)
    fresh_v = current_values.transpose(1, 2, 0, 3)
    score_new = (
        jnp.einsum("rhqd,rhid->rhqi", query_by_group, fresh_k, preferred_element_type=jnp.float32)
        * scale
    )
    new_mask = (
        (jnp.arange(query_rows, dtype=jnp.int32) // query_group_width)[:, None]
        >= jnp.arange(steps, dtype=jnp.int32)[None, :]
    )[None, None]
    fill_new = jnp.where(new_mask, score_new, masked_fill)
    new_max = jnp.max(fill_new, axis=3)
    prob_new = jnp.where(new_mask, jnp.exp(fill_new - new_max[..., None]), 0.0)
    new_weight = jnp.sum(prob_new, axis=3)
    new_acc = jnp.einsum(
        "rhqi,rhid->rhqd",
        prob_new.astype(jnp.bfloat16),
        fresh_v,
        preferred_element_type=jnp.float32,
    )

    lane_pad = ((0, 0), (0, 0), (0, HEAD_SIZE - query_rows))
    packed = jnp.concatenate(
        [
            local_acc,
            jnp.pad(local_max, lane_pad)[:, :, None, :],
            jnp.pad(local_weight, lane_pad)[:, :, None, :],
        ],
        axis=2,
    ).reshape(requests, KEY_HEADS // 2, 2, query_rows + 2, HEAD_SIZE)
    keep = lax.dynamic_index_in_dim(packed, core, axis=2, keepdims=False)
    came = lax.ppermute(
        lax.dynamic_index_in_dim(packed, 1 - core, axis=2, keepdims=False), "core", [(0, 1), (1, 0)]
    )
    keep_max = keep[..., query_rows, :query_rows]
    came_max = came[..., query_rows, :query_rows]
    pair_max = jnp.maximum(keep_max, came_max)
    keep_factor = jnp.exp(keep_max - pair_max)
    came_factor = jnp.exp(came_max - pair_max)
    pair_weight = (
        keep[..., query_rows + 1, :query_rows] * keep_factor
        + came[..., query_rows + 1, :query_rows] * came_factor
    )
    pair_acc = (
        keep[..., :query_rows, :] * keep_factor[..., None]
        + came[..., :query_rows, :] * came_factor[..., None]
    )
    pad_rows = ((0, 0), (0, 0), (0, HEAD_SIZE - query_rows))
    pair_packed = jnp.concatenate(
        [
            pair_acc,
            jnp.pad(pair_max, pad_rows)[:, :, None, :],
            jnp.pad(pair_weight, pad_rows)[:, :, None, :],
        ],
        axis=2,
    ).reshape(seq_count // 2, query_rows + 2, HEAD_SIZE)
    arrived = lax.all_to_all(pair_packed, "z", 0, 0, tiled=True)
    w_out_cols, arrived = lax.optimization_barrier((w_out_cols, arrived))
    part_acc = arrived[:, :query_rows, :]
    part_max = arrived[:, query_rows, :query_rows]
    part_weight = arrived[:, query_rows + 1, :query_rows]
    global_max = jnp.max(part_max, axis=0)
    factor = jnp.exp(part_max - global_max[None])
    global_weight = jnp.sum(part_weight * factor, axis=0)
    global_acc = jnp.sum(part_acc * factor[..., None], axis=0)

    mine_r = seq_index // KEY_HEADS
    mine_h = seq_index % KEY_HEADS
    own_new_max = new_max[mine_r, mine_h]
    own_new_weight = new_weight[mine_r, mine_h]
    own_new_acc = new_acc[mine_r, mine_h]
    top = jnp.maximum(global_max, own_new_max)
    factor_old = jnp.exp(global_max - top)
    factor_new = jnp.exp(own_new_max - top)
    total = global_weight * factor_old + own_new_weight * factor_new
    summed = global_acc * factor_old[..., None] + own_new_acc * factor_new[..., None]
    attention_slice = (summed / total[..., None]).astype(jnp.bfloat16)

    attention_all = lax.all_to_all(
        jnp.broadcast_to(attention_slice[None], (seq_count,) + attention_slice.shape),
        SEQ, 0, 0, tiled=True,
    )
    heads_local = (
        attention_all.reshape(requests, KEY_HEADS, steps, query_group_width, HEAD_SIZE)
        .transpose(2, 0, 1, 3, 4)
        .reshape(steps, requests, query_width)
    )
    owned = jnp.einsum("sbc,cd->sbd", heads_local, w_out_cols, preferred_element_type=jnp.float32)
    return (owned, new_keys, new_values)


def solution(mesh):
    placed = (
        P(None, None, SEQ),
        P(SEQ),
        P(SEQ, "tensor"),
        P("tensor"),
        P("tensor", SEQ),
        P("tensor", SEQ, None),
        P("tensor", SEQ, None),
        P("tensor", SEQ, None),
        P("tensor", SEQ, None),
        P("tensor"),
        P("tensor"),
    )
    planes = jax.sharding.Mesh(
        mesh.devices.reshape(-1, 2, mesh.devices.shape[1]), ("z", "core", "tensor")
    )
    return jax.shard_map(
        body,
        mesh=planes,
        in_specs=placed,
        out_specs=(P(None, "tensor", ("z", "core")), P("tensor", None, None), P("tensor", None, None)),
        check_vma=False,
    )
```

```python
import jax
import jax.numpy as jnp
from jax import lax
from jax.sharding import PartitionSpec as P

D = 5120
QUERY_HEADS = 40
KEY_HEADS = 8
HEAD_SIZE = 128
KEY_COLUMNS = 1024


SEQ = ("z", "core")
epsilon = 1e-06
masked_fill = -1e30


def apply_rotary(values, token_positions):
    half = values.shape[-1] // 2
    freq = jnp.exp(
        -(jnp.arange(half, dtype=jnp.float32) * (2.0 / values.shape[-1]))
        * jnp.log(jnp.float32(1000000.0))
    )
    angles = token_positions[..., None, None] * freq
    cosine = jnp.cos(angles)
    sine = jnp.sin(angles)
    left = values[..., :half]
    right = values[..., half:]
    return jnp.concatenate([left * cosine - right * sine, right * cosine + left * sine], axis=-1)


def body(
    hidden,
    norm_gain,
    w_qkv,
    b_qkv,
    w_out,
    prefix_key_cache,
    prefix_value_cache,
    suffix_key_cache,
    suffix_value_cache,
    prefix_lens,
    suffix_lens,
):
    seq_count = lax.axis_size(SEQ)
    tensor_count = lax.axis_size("tensor")
    steps = hidden.shape[0]
    request_total = hidden.shape[1]
    requests = suffix_lens.shape[0]
    columns = w_qkv.shape[1]
    prefix_count = prefix_key_cache.shape[1]
    suffix_count = suffix_key_cache.shape[1]
    query_group_width = QUERY_HEADS // KEY_HEADS
    query_width = QUERY_HEADS * HEAD_SIZE
    query_rows = steps * query_group_width
    scale = float(HEAD_SIZE) ** (-0.5)
    seq_index = lax.axis_index(SEQ)

    w_out_cols = lax.all_gather(w_out, "tensor", axis=0, tiled=True)

    xf = hidden.astype(jnp.float32)
    local_squares = jnp.sum(xf * xf, axis=2)
    squares = jnp.sum(
        lax.all_to_all(
            jnp.broadcast_to(local_squares[None], (seq_count,) + local_squares.shape),
            SEQ, 0, 0, tiled=True,
        ),
        axis=0,
    )
    normed = (
        xf * lax.rsqrt(squares / D + epsilon)[..., None] * norm_gain.astype(jnp.float32)
    ).astype(jnp.bfloat16)
    partial_value = jnp.einsum("sbd,dc->sbc", normed, w_qkv, preferred_element_type=jnp.float32)

    halves = seq_count // (steps * requests)
    half_width = columns // halves
    groups = request_total // requests
    core = lax.axis_index("core")
    plane_count = seq_count // halves
    partial_value = partial_value + jnp.where(seq_index == 0, b_qkv.astype(jnp.float32), 0.0)
    by_dest = (
        partial_value.reshape(steps, groups, requests, halves, half_width)
        .transpose(3, 1, 0, 2, 4)
        .reshape(halves * groups, steps, requests, half_width)
    )
    came = lax.all_to_all(by_dest, ("core", "tensor"), 0, 0, tiled=True).reshape(
        halves, tensor_count, steps, requests, half_width
    )
    pair_sum = jnp.sum(came, axis=0)
    chunks = pair_sum.transpose(1, 2, 0, 3).reshape(plane_count, tensor_count, half_width)
    owned_rows = jnp.sum(lax.all_to_all(chunks, "z", 0, 0, tiled=True), axis=0)
    gathered = lax.all_gather(owned_rows, SEQ, axis=0, tiled=False)
    combined_output = (
        gathered.reshape(steps, requests, halves, tensor_count, half_width)
        .transpose(0, 1, 3, 2, 4)
        .reshape(steps, requests, tensor_count * columns)
    )

    token_positions = (
        (prefix_lens[0] + suffix_lens)[None, :]
        + jnp.arange(steps, dtype=jnp.int32)[:, None]
    ).astype(jnp.float32)
    query_matrix = apply_rotary(
        combined_output[..., :query_width].reshape(steps, requests, QUERY_HEADS, HEAD_SIZE),
        token_positions,
    ).astype(jnp.bfloat16)
    keys_float = apply_rotary(
        combined_output[..., query_width : query_width + KEY_COLUMNS].reshape(
            steps, requests, KEY_HEADS, HEAD_SIZE
        ),
        token_positions,
    )
    values_float = combined_output[..., query_width + KEY_COLUMNS :].reshape(
        steps, requests, KEY_HEADS, HEAD_SIZE
    )
    current_keys = keys_float.astype(jnp.bfloat16)
    current_values = values_float.astype(jnp.bfloat16)
    new_keys = keys_float.reshape(steps, requests, KEY_COLUMNS).transpose(1, 0, 2)
    new_values = values_float.reshape(steps, requests, KEY_COLUMNS).transpose(1, 0, 2)
    query_by_group = (
        query_matrix.reshape(steps, requests, KEY_HEADS, query_group_width, HEAD_SIZE)
        .transpose(1, 2, 0, 3, 4)
        .reshape(requests, KEY_HEADS, query_rows, HEAD_SIZE)
    )

    prefix_key_block = prefix_key_cache[0].reshape(prefix_count, KEY_HEADS, HEAD_SIZE)
    prefix_value_block = prefix_value_cache[0].reshape(prefix_count, KEY_HEADS, HEAD_SIZE)
    suffix_key_block = suffix_key_cache.reshape(requests, suffix_count, KEY_HEADS, HEAD_SIZE)
    suffix_value_block = suffix_value_cache.reshape(requests, suffix_count, KEY_HEADS, HEAD_SIZE)
    score_pre = (
        jnp.einsum(
            "rhqd,phd->rhqp", query_by_group, prefix_key_block, preferred_element_type=jnp.float32
        )
        * scale
    )
    score_suf = (
        jnp.einsum(
            "rhqd,rshd->rhqs", query_by_group, suffix_key_block, preferred_element_type=jnp.float32
        )
        * scale
    )
    pre_mask = (
        seq_index * prefix_count + jnp.arange(prefix_count, dtype=jnp.int32) < prefix_lens[0]
    )[None, None, None, :]
    suf_mask = (
        (seq_index * suffix_count + jnp.arange(suffix_count, dtype=jnp.int32))[None, :]
        < suffix_lens[:, None]
    )[:, None, None, :]
    fill_pre = jnp.where(pre_mask, score_pre, masked_fill)
    fill_suf = jnp.where(suf_mask, score_suf, masked_fill)
    local_max = jnp.maximum(jnp.max(fill_pre, axis=3), jnp.max(fill_suf, axis=3))
    prob_pre = jnp.where(pre_mask, jnp.exp(fill_pre - local_max[..., None]), 0.0)
    prob_suf = jnp.where(suf_mask, jnp.exp(fill_suf - local_max[..., None]), 0.0)
    local_weight = jnp.sum(prob_pre, axis=3) + jnp.sum(prob_suf, axis=3)
    local_acc = jnp.einsum(
        "rhqp,phd->rhqd",
        prob_pre.astype(jnp.bfloat16),
        prefix_value_block,
        preferred_element_type=jnp.float32,
    )
    local_acc = local_acc + jnp.einsum(
        "rhqs,rshd->rhqd",
        prob_suf.astype(jnp.bfloat16),
        suffix_value_block,
        preferred_element_type=jnp.float32,
    )

    fresh_k = current_keys.transpose(1, 2, 0, 3)
    fresh_v = current_values.transpose(1, 2, 0, 3)
    score_new = (
        jnp.einsum("rhqd,rhid->rhqi", query_by_group, fresh_k, preferred_element_type=jnp.float32)
        * scale
    )
    new_mask = (
        (jnp.arange(query_rows, dtype=jnp.int32) // query_group_width)[:, None]
        >= jnp.arange(steps, dtype=jnp.int32)[None, :]
    )[None, None]
    fill_new = jnp.where(new_mask, score_new, masked_fill)
    new_max = jnp.max(fill_new, axis=3)
    prob_new = jnp.where(new_mask, jnp.exp(fill_new - new_max[..., None]), 0.0)
    new_weight = jnp.sum(prob_new, axis=3)
    new_acc = jnp.einsum(
        "rhqi,rhid->rhqd",
        prob_new.astype(jnp.bfloat16),
        fresh_v,
        preferred_element_type=jnp.float32,
    )

    lane_pad = ((0, 0), (0, 0), (0, HEAD_SIZE - query_rows))
    packed = jnp.concatenate(
        [
            local_acc,
            jnp.pad(local_max, lane_pad)[:, :, None, :],
            jnp.pad(local_weight, lane_pad)[:, :, None, :],
        ],
        axis=2,
    ).reshape(requests, KEY_HEADS // 2, 2, query_rows + 2, HEAD_SIZE)
    keep = lax.dynamic_index_in_dim(packed, core, axis=2, keepdims=False)
    came = lax.ppermute(
        lax.dynamic_index_in_dim(packed, 1 - core, axis=2, keepdims=False), "core", [(0, 1), (1, 0)]
    )
    keep_max = keep[..., query_rows, :query_rows]
    came_max = came[..., query_rows, :query_rows]
    pair_max = jnp.maximum(keep_max, came_max)
    keep_factor = jnp.exp(keep_max - pair_max)
    came_factor = jnp.exp(came_max - pair_max)
    pair_weight = (
        keep[..., query_rows + 1, :query_rows] * keep_factor
        + came[..., query_rows + 1, :query_rows] * came_factor
    )
    pair_acc = (
        keep[..., :query_rows, :] * keep_factor[..., None]
        + came[..., :query_rows, :] * came_factor[..., None]
    )
    pad_rows = ((0, 0), (0, 0), (0, HEAD_SIZE - query_rows))
    pair_packed = jnp.concatenate(
        [
            pair_acc,
            jnp.pad(pair_max, pad_rows)[:, :, None, :],
            jnp.pad(pair_weight, pad_rows)[:, :, None, :],
        ],
        axis=2,
    ).reshape(seq_count // 2, query_rows + 2, HEAD_SIZE)
    arrived = lax.all_to_all(pair_packed, "z", 0, 0, tiled=True)
    w_out_cols, arrived = lax.optimization_barrier((w_out_cols, arrived))
    part_acc = arrived[:, :query_rows, :]
    part_max = arrived[:, query_rows, :query_rows]
    part_weight = arrived[:, query_rows + 1, :query_rows]
    global_max = jnp.max(part_max, axis=0)
    factor = jnp.exp(part_max - global_max[None])
    global_weight = jnp.sum(part_weight * factor, axis=0)
    global_acc = jnp.sum(part_acc * factor[..., None], axis=0)

    mine_r = seq_index // KEY_HEADS
    mine_h = seq_index % KEY_HEADS
    own_new_max = new_max[mine_r, mine_h]
    own_new_weight = new_weight[mine_r, mine_h]
    own_new_acc = new_acc[mine_r, mine_h]
    top = jnp.maximum(global_max, own_new_max)
    factor_old = jnp.exp(global_max - top)
    factor_new = jnp.exp(own_new_max - top)
    total = global_weight * factor_old + own_new_weight * factor_new
    summed = global_acc * factor_old[..., None] + own_new_acc * factor_new[..., None]
    attention_slice = (summed / total[..., None]).astype(jnp.bfloat16)

    attention_all = lax.all_to_all(
        jnp.broadcast_to(attention_slice[None], (seq_count,) + attention_slice.shape),
        SEQ, 0, 0, tiled=True,
    )
    heads_local = (
        attention_all.reshape(requests, KEY_HEADS, steps, query_group_width, HEAD_SIZE)
        .transpose(2, 0, 1, 3, 4)
        .reshape(steps, requests, query_width)
    )
    owned = jnp.einsum("sbc,cd->sbd", heads_local, w_out_cols, preferred_element_type=jnp.float32)
    return (owned, new_keys, new_values)


def solution(mesh):
    placed = (
        P(None, None, SEQ),
        P(SEQ),
        P(SEQ, "tensor"),
        P("tensor"),
        P("tensor", SEQ),
        P("tensor", SEQ, None),
        P("tensor", SEQ, None),
        P("tensor", SEQ, None),
        P("tensor", SEQ, None),
        P("tensor"),
        P("tensor"),
    )
    planes = jax.sharding.Mesh(
        mesh.devices.reshape(-1, 2, mesh.devices.shape[1]), ("z", "core", "tensor")
    )
    return jax.shard_map(
        body,
        mesh=planes,
        in_specs=placed,
        out_specs=(P(None, "tensor", ("z", "core")), P("tensor", None, None), P("tensor", None, None)),
        check_vma=False,
    )
```

```python
import jax
import jax.numpy as jnp
from jax import lax
from jax.sharding import PartitionSpec as P

D = 5120
QUERY_HEADS = 40
KEY_HEADS = 8
HEAD_SIZE = 128
KEY_COLUMNS = 1024


SEQ = ("z", "core")
epsilon = 1e-06
masked_fill = -1e30


def apply_rotary(values, token_positions):
    half = values.shape[-1] // 2
    freq = jnp.exp(
        -(jnp.arange(half, dtype=jnp.float32) * (2.0 / values.shape[-1]))
        * jnp.log(jnp.float32(1000000.0))
    )
    angles = token_positions[..., None, None] * freq
    cosine = jnp.cos(angles)
    sine = jnp.sin(angles)
    left = values[..., :half]
    right = values[..., half:]
    return jnp.concatenate([left * cosine - right * sine, right * cosine + left * sine], axis=-1)


def body(
    hidden,
    norm_gain,
    w_qkv,
    b_qkv,
    w_out,
    prefix_key_cache,
    prefix_value_cache,
    suffix_key_cache,
    suffix_value_cache,
    prefix_lens,
    suffix_lens,
):
    seq_count = lax.axis_size(SEQ)
    tensor_count = lax.axis_size("tensor")
    steps = hidden.shape[0]
    request_total = hidden.shape[1]
    requests = suffix_lens.shape[0]
    columns = w_qkv.shape[1]
    prefix_count = prefix_key_cache.shape[1]
    suffix_count = suffix_key_cache.shape[1]
    query_group_width = QUERY_HEADS // KEY_HEADS
    query_width = QUERY_HEADS * HEAD_SIZE
    query_rows = steps * query_group_width
    scale = float(HEAD_SIZE) ** (-0.5)
    seq_index = lax.axis_index(SEQ)

    w_out_cols = lax.all_gather(w_out, "tensor", axis=0, tiled=True)

    xf = hidden.astype(jnp.float32)
    local_squares = jnp.sum(xf * xf, axis=2)
    squares = jnp.sum(
        lax.all_to_all(
            jnp.broadcast_to(local_squares[None], (seq_count,) + local_squares.shape),
            SEQ, 0, 0, tiled=True,
        ),
        axis=0,
    )
    normed = (
        xf * lax.rsqrt(squares / D + epsilon)[..., None] * norm_gain.astype(jnp.float32)
    ).astype(jnp.bfloat16)
    partial_value = jnp.einsum("sbd,dc->sbc", normed, w_qkv, preferred_element_type=jnp.float32)

    halves = seq_count // (steps * requests)
    half_width = columns // halves
    groups = request_total // requests
    core = lax.axis_index("core")
    plane_count = seq_count // halves
    by_half = partial_value.reshape(steps, groups, requests, halves, half_width)
    keep = lax.dynamic_index_in_dim(by_half, core, axis=3, keepdims=False)
    send = lax.dynamic_index_in_dim(by_half, 1 - core, axis=3, keepdims=False)
    pair_sum = keep + lax.ppermute(send, "core", [(0, 1), (1, 0)])
    chunks = pair_sum.transpose(0, 2, 1, 3).reshape(plane_count, groups, half_width)
    reduced = jnp.sum(lax.all_to_all(chunks, "z", 0, 0, tiled=True), axis=0)
    bias = lax.dynamic_slice_in_dim(
        b_qkv.astype(jnp.float32), (seq_index % halves) * half_width, half_width
    )
    reduced = reduced + bias[None, :]
    owned_rows = lax.all_to_all(reduced, "tensor", 0, 0, tiled=True)
    gathered = (
        lax.all_gather(owned_rows, ("core", "z"), axis=0, tiled=False)
        .reshape((2, seq_count // 2) + owned_rows.shape)
        .transpose(1, 0, 2, 3)
    )
    combined_output = (
        gathered.reshape(steps, requests, halves, tensor_count, half_width)
        .transpose(0, 1, 3, 2, 4)
        .reshape(steps, requests, tensor_count * columns)
    )

    token_positions = (
        (prefix_lens[0] + suffix_lens)[None, :]
        + jnp.arange(steps, dtype=jnp.int32)[:, None]
    ).astype(jnp.float32)
    query_matrix = apply_rotary(
        combined_output[..., :query_width].reshape(steps, requests, QUERY_HEADS, HEAD_SIZE),
        token_positions,
    ).astype(jnp.bfloat16)
    keys_float = apply_rotary(
        combined_output[..., query_width : query_width + KEY_COLUMNS].reshape(
            steps, requests, KEY_HEADS, HEAD_SIZE
        ),
        token_positions,
    )
    values_float = combined_output[..., query_width + KEY_COLUMNS :].reshape(
        steps, requests, KEY_HEADS, HEAD_SIZE
    )
    current_keys = keys_float.astype(jnp.bfloat16)
    current_values = values_float.astype(jnp.bfloat16)
    new_keys = keys_float.reshape(steps, requests, KEY_COLUMNS).transpose(1, 0, 2)
    new_values = values_float.reshape(steps, requests, KEY_COLUMNS).transpose(1, 0, 2)
    query_by_group = (
        query_matrix.reshape(steps, requests, KEY_HEADS, query_group_width, HEAD_SIZE)
        .transpose(1, 2, 0, 3, 4)
        .reshape(requests, KEY_HEADS, query_rows, HEAD_SIZE)
    )

    prefix_key_block = prefix_key_cache[0].reshape(prefix_count, KEY_HEADS, HEAD_SIZE)
    prefix_value_block = prefix_value_cache[0].reshape(prefix_count, KEY_HEADS, HEAD_SIZE)
    suffix_key_block = suffix_key_cache.reshape(requests, suffix_count, KEY_HEADS, HEAD_SIZE)
    suffix_value_block = suffix_value_cache.reshape(requests, suffix_count, KEY_HEADS, HEAD_SIZE)
    score_pre = (
        jnp.einsum(
            "rhqd,phd->rhqp", query_by_group, prefix_key_block, preferred_element_type=jnp.float32
        )
        * scale
    )
    score_suf = (
        jnp.einsum(
            "rhqd,rshd->rhqs", query_by_group, suffix_key_block, preferred_element_type=jnp.float32
        )
        * scale
    )
    pre_mask = (
        seq_index * prefix_count + jnp.arange(prefix_count, dtype=jnp.int32) < prefix_lens[0]
    )[None, None, None, :]
    suf_mask = (
        (seq_index * suffix_count + jnp.arange(suffix_count, dtype=jnp.int32))[None, :]
        < suffix_lens[:, None]
    )[:, None, None, :]
    fill_pre = jnp.where(pre_mask, score_pre, masked_fill)
    fill_suf = jnp.where(suf_mask, score_suf, masked_fill)
    local_max = jnp.maximum(jnp.max(fill_pre, axis=3), jnp.max(fill_suf, axis=3))
    prob_pre = jnp.where(pre_mask, jnp.exp(fill_pre - local_max[..., None]), 0.0)
    prob_suf = jnp.where(suf_mask, jnp.exp(fill_suf - local_max[..., None]), 0.0)
    local_weight = jnp.sum(prob_pre, axis=3) + jnp.sum(prob_suf, axis=3)
    local_acc = jnp.einsum(
        "rhqp,phd->rhqd",
        prob_pre.astype(jnp.bfloat16),
        prefix_value_block,
        preferred_element_type=jnp.float32,
    )
    local_acc = local_acc + jnp.einsum(
        "rhqs,rshd->rhqd",
        prob_suf.astype(jnp.bfloat16),
        suffix_value_block,
        preferred_element_type=jnp.float32,
    )

    fresh_k = current_keys.transpose(1, 2, 0, 3)
    fresh_v = current_values.transpose(1, 2, 0, 3)
    score_new = (
        jnp.einsum("rhqd,rhid->rhqi", query_by_group, fresh_k, preferred_element_type=jnp.float32)
        * scale
    )
    new_mask = (
        (jnp.arange(query_rows, dtype=jnp.int32) // query_group_width)[:, None]
        >= jnp.arange(steps, dtype=jnp.int32)[None, :]
    )[None, None]
    fill_new = jnp.where(new_mask, score_new, masked_fill)
    new_max = jnp.max(fill_new, axis=3)
    prob_new = jnp.where(new_mask, jnp.exp(fill_new - new_max[..., None]), 0.0)
    new_weight = jnp.sum(prob_new, axis=3)
    new_acc = jnp.einsum(
        "rhqi,rhid->rhqd",
        prob_new.astype(jnp.bfloat16),
        fresh_v,
        preferred_element_type=jnp.float32,
    )

    lane_pad = ((0, 0), (0, 0), (0, HEAD_SIZE - query_rows))
    packed = jnp.concatenate(
        [
            local_acc,
            jnp.pad(local_max, lane_pad)[:, :, None, :],
            jnp.pad(local_weight, lane_pad)[:, :, None, :],
        ],
        axis=2,
    ).reshape(requests, KEY_HEADS // 2, 2, query_rows + 2, HEAD_SIZE)
    keep = lax.dynamic_index_in_dim(packed, core, axis=2, keepdims=False)
    came = lax.ppermute(
        lax.dynamic_index_in_dim(packed, 1 - core, axis=2, keepdims=False), "core", [(0, 1), (1, 0)]
    )
    keep_max = keep[..., query_rows, :query_rows]
    came_max = came[..., query_rows, :query_rows]
    pair_max = jnp.maximum(keep_max, came_max)
    keep_factor = jnp.exp(keep_max - pair_max)
    came_factor = jnp.exp(came_max - pair_max)
    pair_weight = (
        keep[..., query_rows + 1, :query_rows] * keep_factor
        + came[..., query_rows + 1, :query_rows] * came_factor
    )
    pair_acc = (
        keep[..., :query_rows, :] * keep_factor[..., None]
        + came[..., :query_rows, :] * came_factor[..., None]
    )
    pad_rows = ((0, 0), (0, 0), (0, HEAD_SIZE - query_rows))
    pair_packed = jnp.concatenate(
        [
            pair_acc,
            jnp.pad(pair_max, pad_rows)[:, :, None, :],
            jnp.pad(pair_weight, pad_rows)[:, :, None, :],
        ],
        axis=2,
    ).reshape(seq_count // 2, query_rows + 2, HEAD_SIZE)
    arrived = lax.all_to_all(pair_packed, "z", 0, 0, tiled=True)
    w_out_cols, arrived = lax.optimization_barrier((w_out_cols, arrived))
    part_acc = arrived[:, :query_rows, :]
    part_max = arrived[:, query_rows, :query_rows]
    part_weight = arrived[:, query_rows + 1, :query_rows]
    global_max = jnp.max(part_max, axis=0)
    factor = jnp.exp(part_max - global_max[None])
    global_weight = jnp.sum(part_weight * factor, axis=0)
    global_acc = jnp.sum(part_acc * factor[..., None], axis=0)

    mine_r = seq_index // KEY_HEADS
    mine_h = seq_index % KEY_HEADS
    own_new_max = new_max[mine_r, mine_h]
    own_new_weight = new_weight[mine_r, mine_h]
    own_new_acc = new_acc[mine_r, mine_h]
    top = jnp.maximum(global_max, own_new_max)
    factor_old = jnp.exp(global_max - top)
    factor_new = jnp.exp(own_new_max - top)
    total = global_weight * factor_old + own_new_weight * factor_new
    summed = global_acc * factor_old[..., None] + own_new_acc * factor_new[..., None]
    attention_slice = (summed / total[..., None]).astype(jnp.bfloat16)

    attention_all = lax.all_to_all(
        jnp.broadcast_to(attention_slice[None], (seq_count,) + attention_slice.shape),
        SEQ, 0, 0, tiled=True,
    )
    heads_local = (
        attention_all.reshape(requests, KEY_HEADS, steps, query_group_width, HEAD_SIZE)
        .transpose(2, 0, 1, 3, 4)
        .reshape(steps, requests, query_width)
    )
    owned = jnp.einsum("sbc,cd->sbd", heads_local, w_out_cols, preferred_element_type=jnp.float32)
    return (owned, new_keys, new_values)


def solution(mesh):
    placed = (
        P(None, None, SEQ),
        P(SEQ),
        P(SEQ, "tensor"),
        P("tensor"),
        P("tensor", SEQ),
        P("tensor", SEQ, None),
        P("tensor", SEQ, None),
        P("tensor", SEQ, None),
        P("tensor", SEQ, None),
        P("tensor"),
        P("tensor"),
    )
    planes = jax.sharding.Mesh(
        mesh.devices.reshape(-1, 2, mesh.devices.shape[1]), ("z", "core", "tensor")
    )
    return jax.shard_map(
        body,
        mesh=planes,
        in_specs=placed,
        out_specs=(P(None, "tensor", ("z", "core")), P("tensor", None, None), P("tensor", None, None)),
        check_vma=False,
    )
```

```python
import jax
import jax.numpy as jnp
from jax import lax
from jax.sharding import PartitionSpec as P

D = 5120
QUERY_HEADS = 40
KEY_HEADS = 8
HEAD_SIZE = 128
KEY_COLUMNS = 1024


SEQ = ("z", "core")
epsilon = 1e-06
masked_fill = -1e30


def apply_rotary(values, token_positions):
    half = values.shape[-1] // 2
    freq = jnp.exp(
        -(jnp.arange(half, dtype=jnp.float32) * (2.0 / values.shape[-1]))
        * jnp.log(jnp.float32(1000000.0))
    )
    angles = token_positions[..., None, None] * freq
    cosine = jnp.cos(angles)
    sine = jnp.sin(angles)
    left = values[..., :half]
    right = values[..., half:]
    return jnp.concatenate([left * cosine - right * sine, right * cosine + left * sine], axis=-1)


def body(
    hidden,
    norm_gain,
    w_qkv,
    b_qkv,
    w_out,
    prefix_key_cache,
    prefix_value_cache,
    suffix_key_cache,
    suffix_value_cache,
    prefix_lens,
    suffix_lens,
):
    seq_count = lax.axis_size(SEQ)
    tensor_count = lax.axis_size("tensor")
    steps = hidden.shape[0]
    request_total = hidden.shape[1]
    requests = suffix_lens.shape[0]
    columns = w_qkv.shape[1]
    prefix_count = prefix_key_cache.shape[1]
    suffix_count = suffix_key_cache.shape[1]
    query_group_width = QUERY_HEADS // KEY_HEADS
    query_width = QUERY_HEADS * HEAD_SIZE
    query_rows = steps * query_group_width
    scale = float(HEAD_SIZE) ** (-0.5)
    seq_index = lax.axis_index(SEQ)

    w_out_cols = lax.all_gather(w_out, "tensor", axis=0, tiled=True)

    xf = hidden.astype(jnp.float32)
    local_squares = jnp.sum(xf * xf, axis=2)
    squares = jnp.sum(
        lax.all_to_all(
            jnp.broadcast_to(local_squares[None], (seq_count,) + local_squares.shape),
            SEQ, 0, 0, tiled=True,
        ),
        axis=0,
    )
    normed = (
        xf * lax.rsqrt(squares / D + epsilon)[..., None] * norm_gain.astype(jnp.float32)
    ).astype(jnp.bfloat16)
    partial_value = jnp.einsum("sbd,dc->sbc", normed, w_qkv, preferred_element_type=jnp.float32)

    halves = seq_count // (steps * requests)
    half_width = columns // halves
    groups = request_total // requests
    core = lax.axis_index("core")
    plane_count = seq_count // halves
    by_half = partial_value.reshape(steps, groups, requests, halves, half_width)
    keep = lax.dynamic_index_in_dim(by_half, core, axis=3, keepdims=False)
    send = lax.dynamic_index_in_dim(by_half, 1 - core, axis=3, keepdims=False)
    pair_sum = keep + lax.ppermute(send, "core", [(0, 1), (1, 0)])
    chunks = pair_sum.transpose(0, 2, 1, 3).reshape(plane_count, groups, half_width)
    reduced = jnp.sum(lax.all_to_all(chunks, "z", 0, 0, tiled=True), axis=0)
    bias = lax.dynamic_slice_in_dim(
        b_qkv.astype(jnp.float32), (seq_index % halves) * half_width, half_width
    )
    reduced = reduced + bias[None, :]
    owned_rows = lax.all_to_all(reduced, "tensor", 0, 0, tiled=True)
    gathered = lax.all_gather(owned_rows.reshape(1, -1), SEQ, axis=0, tiled=True)
    combined_output = (
        gathered.reshape(steps, requests, halves, tensor_count, half_width)
        .transpose(0, 1, 3, 2, 4)
        .reshape(steps, requests, tensor_count * columns)
    )

    token_positions = (
        (prefix_lens[0] + suffix_lens)[None, :]
        + jnp.arange(steps, dtype=jnp.int32)[:, None]
    ).astype(jnp.float32)
    query_matrix = apply_rotary(
        combined_output[..., :query_width].reshape(steps, requests, QUERY_HEADS, HEAD_SIZE),
        token_positions,
    ).astype(jnp.bfloat16)
    keys_float = apply_rotary(
        combined_output[..., query_width : query_width + KEY_COLUMNS].reshape(
            steps, requests, KEY_HEADS, HEAD_SIZE
        ),
        token_positions,
    )
    values_float = combined_output[..., query_width + KEY_COLUMNS :].reshape(
        steps, requests, KEY_HEADS, HEAD_SIZE
    )
    current_keys = keys_float.astype(jnp.bfloat16)
    current_values = values_float.astype(jnp.bfloat16)
    new_keys = keys_float.reshape(steps, requests, KEY_COLUMNS).transpose(1, 0, 2)
    new_values = values_float.reshape(steps, requests, KEY_COLUMNS).transpose(1, 0, 2)
    query_by_group = (
        query_matrix.reshape(steps, requests, KEY_HEADS, query_group_width, HEAD_SIZE)
        .transpose(1, 2, 0, 3, 4)
        .reshape(requests, KEY_HEADS, query_rows, HEAD_SIZE)
    )

    prefix_key_block = prefix_key_cache[0].reshape(prefix_count, KEY_HEADS, HEAD_SIZE)
    prefix_value_block = prefix_value_cache[0].reshape(prefix_count, KEY_HEADS, HEAD_SIZE)
    suffix_key_block = suffix_key_cache.reshape(requests, suffix_count, KEY_HEADS, HEAD_SIZE)
    suffix_value_block = suffix_value_cache.reshape(requests, suffix_count, KEY_HEADS, HEAD_SIZE)
    score_pre = (
        jnp.einsum(
            "rhqd,phd->rhqp", query_by_group, prefix_key_block, preferred_element_type=jnp.float32
        )
        * scale
    )
    score_suf = (
        jnp.einsum(
            "rhqd,rshd->rhqs", query_by_group, suffix_key_block, preferred_element_type=jnp.float32
        )
        * scale
    )
    pre_mask = (
        seq_index * prefix_count + jnp.arange(prefix_count, dtype=jnp.int32) < prefix_lens[0]
    )[None, None, None, :]
    suf_mask = (
        (seq_index * suffix_count + jnp.arange(suffix_count, dtype=jnp.int32))[None, :]
        < suffix_lens[:, None]
    )[:, None, None, :]
    fill_pre = jnp.where(pre_mask, score_pre, masked_fill)
    fill_suf = jnp.where(suf_mask, score_suf, masked_fill)
    local_max = jnp.maximum(jnp.max(fill_pre, axis=3), jnp.max(fill_suf, axis=3))
    prob_pre = jnp.where(pre_mask, jnp.exp(fill_pre - local_max[..., None]), 0.0)
    prob_suf = jnp.where(suf_mask, jnp.exp(fill_suf - local_max[..., None]), 0.0)
    local_weight = jnp.sum(prob_pre, axis=3) + jnp.sum(prob_suf, axis=3)
    local_acc = jnp.einsum(
        "rhqp,phd->rhqd",
        prob_pre.astype(jnp.bfloat16),
        prefix_value_block,
        preferred_element_type=jnp.float32,
    )
    local_acc = local_acc + jnp.einsum(
        "rhqs,rshd->rhqd",
        prob_suf.astype(jnp.bfloat16),
        suffix_value_block,
        preferred_element_type=jnp.float32,
    )

    fresh_k = current_keys.transpose(1, 2, 0, 3)
    fresh_v = current_values.transpose(1, 2, 0, 3)
    score_new = (
        jnp.einsum("rhqd,rhid->rhqi", query_by_group, fresh_k, preferred_element_type=jnp.float32)
        * scale
    )
    new_mask = (
        (jnp.arange(query_rows, dtype=jnp.int32) // query_group_width)[:, None]
        >= jnp.arange(steps, dtype=jnp.int32)[None, :]
    )[None, None]
    fill_new = jnp.where(new_mask, score_new, masked_fill)
    new_max = jnp.max(fill_new, axis=3)
    prob_new = jnp.where(new_mask, jnp.exp(fill_new - new_max[..., None]), 0.0)
    new_weight = jnp.sum(prob_new, axis=3)
    new_acc = jnp.einsum(
        "rhqi,rhid->rhqd",
        prob_new.astype(jnp.bfloat16),
        fresh_v,
        preferred_element_type=jnp.float32,
    )

    lane_pad = ((0, 0), (0, 0), (0, HEAD_SIZE - query_rows))
    packed = jnp.concatenate(
        [
            local_acc,
            jnp.pad(local_max, lane_pad)[:, :, None, :],
            jnp.pad(local_weight, lane_pad)[:, :, None, :],
        ],
        axis=2,
    ).reshape(requests, KEY_HEADS // 2, 2, query_rows + 2, HEAD_SIZE)
    keep = lax.dynamic_index_in_dim(packed, core, axis=2, keepdims=False)
    came = lax.ppermute(
        lax.dynamic_index_in_dim(packed, 1 - core, axis=2, keepdims=False), "core", [(0, 1), (1, 0)]
    )
    keep_max = keep[..., query_rows, :query_rows]
    came_max = came[..., query_rows, :query_rows]
    pair_max = jnp.maximum(keep_max, came_max)
    keep_factor = jnp.exp(keep_max - pair_max)
    came_factor = jnp.exp(came_max - pair_max)
    pair_weight = (
        keep[..., query_rows + 1, :query_rows] * keep_factor
        + came[..., query_rows + 1, :query_rows] * came_factor
    )
    pair_acc = (
        keep[..., :query_rows, :] * keep_factor[..., None]
        + came[..., :query_rows, :] * came_factor[..., None]
    )
    pad_rows = ((0, 0), (0, 0), (0, HEAD_SIZE - query_rows))
    pair_packed = jnp.concatenate(
        [
            pair_acc,
            jnp.pad(pair_max, pad_rows)[:, :, None, :],
            jnp.pad(pair_weight, pad_rows)[:, :, None, :],
        ],
        axis=2,
    ).reshape(seq_count // 2, query_rows + 2, HEAD_SIZE)
    arrived = lax.all_to_all(pair_packed, "z", 0, 0, tiled=True)
    w_out_cols, arrived = lax.optimization_barrier((w_out_cols, arrived))
    part_acc = arrived[:, :query_rows, :]
    part_max = arrived[:, query_rows, :query_rows]
    part_weight = arrived[:, query_rows + 1, :query_rows]
    global_max = jnp.max(part_max, axis=0)
    factor = jnp.exp(part_max - global_max[None])
    global_weight = jnp.sum(part_weight * factor, axis=0)
    global_acc = jnp.sum(part_acc * factor[..., None], axis=0)

    mine_r = seq_index // KEY_HEADS
    mine_h = seq_index % KEY_HEADS
    own_new_max = new_max[mine_r, mine_h]
    own_new_weight = new_weight[mine_r, mine_h]
    own_new_acc = new_acc[mine_r, mine_h]
    top = jnp.maximum(global_max, own_new_max)
    factor_old = jnp.exp(global_max - top)
    factor_new = jnp.exp(own_new_max - top)
    total = global_weight * factor_old + own_new_weight * factor_new
    summed = global_acc * factor_old[..., None] + own_new_acc * factor_new[..., None]
    attention_slice = (summed / total[..., None]).astype(jnp.bfloat16)

    attention_all = lax.all_to_all(
        jnp.broadcast_to(attention_slice[None], (seq_count,) + attention_slice.shape),
        SEQ, 0, 0, tiled=True,
    )
    heads_local = (
        attention_all.reshape(requests, KEY_HEADS, steps, query_group_width, HEAD_SIZE)
        .transpose(2, 0, 1, 3, 4)
        .reshape(steps, requests, query_width)
    )
    owned = jnp.einsum("sbc,cd->sbd", heads_local, w_out_cols, preferred_element_type=jnp.float32)
    return (owned, new_keys, new_values)


def solution(mesh):
    placed = (
        P(None, None, SEQ),
        P(SEQ),
        P(SEQ, "tensor"),
        P("tensor"),
        P("tensor", SEQ),
        P("tensor", SEQ, None),
        P("tensor", SEQ, None),
        P("tensor", SEQ, None),
        P("tensor", SEQ, None),
        P("tensor"),
        P("tensor"),
    )
    planes = jax.sharding.Mesh(
        mesh.devices.reshape(-1, 2, mesh.devices.shape[1]), ("z", "core", "tensor")
    )
    return jax.shard_map(
        body,
        mesh=planes,
        in_specs=placed,
        out_specs=(P(None, "tensor", ("z", "core")), P("tensor", None, None), P("tensor", None, None)),
        check_vma=False,
    )
```

```python
import jax
import jax.numpy as jnp
from jax import lax
from jax.sharding import PartitionSpec as P

D = 5120
QUERY_HEADS = 40
KEY_HEADS = 8
HEAD_SIZE = 128
KEY_COLUMNS = 1024


SEQ = ("z", "core")
epsilon = 1e-06
masked_fill = -1e30


def apply_rotary(values, token_positions):
    half = values.shape[-1] // 2
    freq = jnp.exp(
        -(jnp.arange(half, dtype=jnp.float32) * (2.0 / values.shape[-1]))
        * jnp.log(jnp.float32(1000000.0))
    )
    angles = token_positions[..., None, None] * freq
    cosine = jnp.cos(angles)
    sine = jnp.sin(angles)
    left = values[..., :half]
    right = values[..., half:]
    return jnp.concatenate([left * cosine - right * sine, right * cosine + left * sine], axis=-1)


def body(
    hidden,
    norm_gain,
    w_qkv,
    b_qkv,
    w_out,
    prefix_key_cache,
    prefix_value_cache,
    suffix_key_cache,
    suffix_value_cache,
    prefix_lens,
    suffix_lens,
):
    seq_count = lax.axis_size(SEQ)
    tensor_count = lax.axis_size("tensor")
    steps = hidden.shape[0]
    request_total = hidden.shape[1]
    requests = suffix_lens.shape[0]
    columns = w_qkv.shape[1]
    prefix_count = prefix_key_cache.shape[1]
    suffix_count = suffix_key_cache.shape[1]
    query_group_width = QUERY_HEADS // KEY_HEADS
    query_width = QUERY_HEADS * HEAD_SIZE
    query_rows = steps * query_group_width
    scale = float(HEAD_SIZE) ** (-0.5)
    seq_index = lax.axis_index(SEQ)

    w_out_cols = lax.all_gather(w_out, "tensor", axis=0, tiled=True)

    xf = hidden.astype(jnp.float32)
    local_squares = jnp.sum(xf * xf, axis=2)
    squares = jnp.sum(
        lax.all_to_all(
            jnp.broadcast_to(local_squares[None], (seq_count,) + local_squares.shape),
            SEQ, 0, 0, tiled=True,
        ),
        axis=0,
    )
    normed = (
        xf * lax.rsqrt(squares / D + epsilon)[..., None] * norm_gain.astype(jnp.float32)
    ).astype(jnp.bfloat16)
    partial_value = jnp.einsum("sbd,dc->sbc", normed, w_qkv, preferred_element_type=jnp.float32)

    halves = seq_count // (steps * requests)
    half_width = columns // halves
    groups = request_total // requests
    core = lax.axis_index("core")
    plane_count = seq_count // halves
    by_half = partial_value.reshape(steps, groups, requests, halves, half_width)
    keep = lax.dynamic_index_in_dim(by_half, core, axis=3, keepdims=False)
    send = lax.dynamic_index_in_dim(by_half, 1 - core, axis=3, keepdims=False)
    pair_sum = keep + lax.ppermute(send, "core", [(0, 1), (1, 0)])
    chunks = pair_sum.transpose(0, 2, 1, 3).reshape(plane_count, groups, half_width)
    reduced = jnp.sum(lax.all_to_all(chunks, "z", 0, 0, tiled=True), axis=0)
    bias = lax.dynamic_slice_in_dim(
        b_qkv.astype(jnp.float32), (seq_index % halves) * half_width, half_width
    )
    reduced = reduced + bias[None, :]
    owned_rows = lax.all_to_all(reduced, "tensor", 0, 0, tiled=True)
    gathered = lax.all_gather(owned_rows, SEQ, axis=0, tiled=False)
    combined_output = (
        gathered.reshape(steps, requests, halves, tensor_count, half_width)
        .transpose(0, 1, 3, 2, 4)
        .reshape(steps, requests, tensor_count * columns)
    )

    token_positions = (
        (prefix_lens[0] + suffix_lens)[None, :]
        + jnp.arange(steps, dtype=jnp.int32)[:, None]
    ).astype(jnp.float32)
    query_matrix = apply_rotary(
        combined_output[..., :query_width].reshape(steps, requests, QUERY_HEADS, HEAD_SIZE),
        token_positions,
    ).astype(jnp.bfloat16)
    keys_float = apply_rotary(
        combined_output[..., query_width : query_width + KEY_COLUMNS].reshape(
            steps, requests, KEY_HEADS, HEAD_SIZE
        ),
        token_positions,
    )
    values_float = combined_output[..., query_width + KEY_COLUMNS :].reshape(
        steps, requests, KEY_HEADS, HEAD_SIZE
    )
    current_keys = keys_float.astype(jnp.bfloat16)
    current_values = values_float.astype(jnp.bfloat16)
    new_keys = keys_float.reshape(steps, requests, KEY_COLUMNS).transpose(1, 0, 2)
    new_values = values_float.reshape(steps, requests, KEY_COLUMNS).transpose(1, 0, 2)
    query_by_group = (
        query_matrix.reshape(steps, requests, KEY_HEADS, query_group_width, HEAD_SIZE)
        .transpose(1, 2, 0, 3, 4)
        .reshape(requests, KEY_HEADS, query_rows, HEAD_SIZE)
    )

    prefix_key_block = prefix_key_cache[0].reshape(prefix_count, KEY_HEADS, HEAD_SIZE)
    prefix_value_block = prefix_value_cache[0].reshape(prefix_count, KEY_HEADS, HEAD_SIZE)
    suffix_key_block = suffix_key_cache.reshape(requests, suffix_count, KEY_HEADS, HEAD_SIZE)
    suffix_value_block = suffix_value_cache.reshape(requests, suffix_count, KEY_HEADS, HEAD_SIZE)
    score_pre = (
        jnp.einsum(
            "rhqd,phd->rhqp", query_by_group, prefix_key_block, preferred_element_type=jnp.float32
        )
        * scale
    )
    score_suf = (
        jnp.einsum(
            "rhqd,rshd->rhqs", query_by_group, suffix_key_block, preferred_element_type=jnp.float32
        )
        * scale
    )
    pre_mask = (
        seq_index * prefix_count + jnp.arange(prefix_count, dtype=jnp.int32) < prefix_lens[0]
    )[None, None, None, :]
    suf_mask = (
        (seq_index * suffix_count + jnp.arange(suffix_count, dtype=jnp.int32))[None, :]
        < suffix_lens[:, None]
    )[:, None, None, :]
    fill_pre = jnp.where(pre_mask, score_pre, masked_fill)
    fill_suf = jnp.where(suf_mask, score_suf, masked_fill)
    local_max = jnp.maximum(jnp.max(fill_pre, axis=3), jnp.max(fill_suf, axis=3))
    prob_pre = jnp.where(pre_mask, jnp.exp(fill_pre - local_max[..., None]), 0.0)
    prob_suf = jnp.where(suf_mask, jnp.exp(fill_suf - local_max[..., None]), 0.0)
    local_weight = jnp.sum(prob_pre, axis=3) + jnp.sum(prob_suf, axis=3)
    local_acc = jnp.einsum(
        "rhqp,phd->rhqd",
        prob_pre.astype(jnp.bfloat16),
        prefix_value_block,
        preferred_element_type=jnp.float32,
    )
    local_acc = local_acc + jnp.einsum(
        "rhqs,rshd->rhqd",
        prob_suf.astype(jnp.bfloat16),
        suffix_value_block,
        preferred_element_type=jnp.float32,
    )

    fresh_k = current_keys.transpose(1, 2, 0, 3)
    fresh_v = current_values.transpose(1, 2, 0, 3)
    score_new = (
        jnp.einsum("rhqd,rhid->rhqi", query_by_group, fresh_k, preferred_element_type=jnp.float32)
        * scale
    )
    new_mask = (
        (jnp.arange(query_rows, dtype=jnp.int32) // query_group_width)[:, None]
        >= jnp.arange(steps, dtype=jnp.int32)[None, :]
    )[None, None]
    fill_new = jnp.where(new_mask, score_new, masked_fill)
    new_max = jnp.max(fill_new, axis=3)
    prob_new = jnp.where(new_mask, jnp.exp(fill_new - new_max[..., None]), 0.0)
    new_weight = jnp.sum(prob_new, axis=3)
    new_acc = jnp.einsum(
        "rhqi,rhid->rhqd",
        prob_new.astype(jnp.bfloat16),
        fresh_v,
        preferred_element_type=jnp.float32,
    )

    lane_pad = ((0, 0), (0, 0), (0, HEAD_SIZE - query_rows))
    packed = jnp.concatenate(
        [
            local_acc,
            jnp.pad(local_max, lane_pad)[:, :, None, :],
            jnp.pad(local_weight, lane_pad)[:, :, None, :],
        ],
        axis=2,
    ).reshape(requests, KEY_HEADS // 2, 2, query_rows + 2, HEAD_SIZE)
    keep = lax.dynamic_index_in_dim(packed, core, axis=2, keepdims=False)
    came = lax.ppermute(
        lax.dynamic_index_in_dim(packed, 1 - core, axis=2, keepdims=False), "core", [(0, 1), (1, 0)]
    )
    keep_max = keep[..., query_rows, :query_rows]
    came_max = came[..., query_rows, :query_rows]
    pair_max = jnp.maximum(keep_max, came_max)
    keep_factor = jnp.exp(keep_max - pair_max)
    came_factor = jnp.exp(came_max - pair_max)
    pair_weight = (
        keep[..., query_rows + 1, :query_rows] * keep_factor
        + came[..., query_rows + 1, :query_rows] * came_factor
    )
    pair_acc = (
        keep[..., :query_rows, :] * keep_factor[..., None]
        + came[..., :query_rows, :] * came_factor[..., None]
    )
    pad_rows = ((0, 0), (0, 0), (0, HEAD_SIZE - query_rows))
    pair_packed = jnp.concatenate(
        [
            pair_acc,
            jnp.pad(pair_max, pad_rows)[:, :, None, :],
            jnp.pad(pair_weight, pad_rows)[:, :, None, :],
        ],
        axis=2,
    ).reshape(seq_count // 2, query_rows + 2, HEAD_SIZE)
    arrived = lax.all_to_all(pair_packed, "z", 0, 0, tiled=True)
    w_out_cols, arrived = lax.optimization_barrier((w_out_cols, arrived))
    part_acc = arrived[:, :query_rows, :]
    part_max = arrived[:, query_rows, :query_rows]
    part_weight = arrived[:, query_rows + 1, :query_rows]
    global_max = jnp.max(part_max, axis=0)
    factor = jnp.exp(part_max - global_max[None])
    global_weight = jnp.sum(part_weight * factor, axis=0)
    global_acc = jnp.sum(part_acc * factor[..., None], axis=0)

    mine_r = seq_index // KEY_HEADS
    mine_h = seq_index % KEY_HEADS
    own_new_max = new_max[mine_r, mine_h]
    own_new_weight = new_weight[mine_r, mine_h]
    own_new_acc = new_acc[mine_r, mine_h]
    top = jnp.maximum(global_max, own_new_max)
    factor_old = jnp.exp(global_max - top)
    factor_new = jnp.exp(own_new_max - top)
    total = global_weight * factor_old + own_new_weight * factor_new
    summed = global_acc * factor_old[..., None] + own_new_acc * factor_new[..., None]
    attention_slice = (summed / total[..., None]).astype(jnp.bfloat16)

    flat_slice = attention_slice.reshape(1, -1)
    attention_all = lax.all_to_all(
        jnp.broadcast_to(flat_slice[None], (seq_count,) + flat_slice.shape), SEQ, 0, 0, tiled=True
    ).reshape((seq_count,) + attention_slice.shape)
    heads_local = (
        attention_all.reshape(requests, KEY_HEADS, steps, query_group_width, HEAD_SIZE)
        .transpose(2, 0, 1, 3, 4)
        .reshape(steps, requests, query_width)
    )
    owned = jnp.einsum("sbc,cd->sbd", heads_local, w_out_cols, preferred_element_type=jnp.float32)
    return (owned, new_keys, new_values)


def solution(mesh):
    placed = (
        P(None, None, SEQ),
        P(SEQ),
        P(SEQ, "tensor"),
        P("tensor"),
        P("tensor", SEQ),
        P("tensor", SEQ, None),
        P("tensor", SEQ, None),
        P("tensor", SEQ, None),
        P("tensor", SEQ, None),
        P("tensor"),
        P("tensor"),
    )
    planes = jax.sharding.Mesh(
        mesh.devices.reshape(-1, 2, mesh.devices.shape[1]), ("z", "core", "tensor")
    )
    return jax.shard_map(
        body,
        mesh=planes,
        in_specs=placed,
        out_specs=(P(None, "tensor", ("z", "core")), P("tensor", None, None), P("tensor", None, None)),
        check_vma=False,
    )
```
